32 devices in a mesh: stream: 2 (over y), dev: 16 (over z, x, core).
Axes of the slice: x: 2, y: 2, z: 4, core: 2. Of those that a mesh axis runs over, the one named last changes fastest.
Arguments:
- latents: bfloat16 [32, 2, 3, 16, 1664], P(('stream', 'dev')), parts along dimension 0, may hold values from -6 to 6
- owners: int32 [4], P('stream'), parts along dimension 0, may hold values from 0 to 15
- conv_in: bfloat16 [432, 384], replicated, may hold values from -0.3125 to 0.3125
- conv_mid: bfloat16 [10368, 384], replicated, may hold values from -0.0625 to 0.0625
- to_pixels: bfloat16 [384, 12], replicated, may hold values from -0.3125 to 0.3125
Outputs:
- pixels: bfloat16 [4, 3, 32, 624], P('stream', None, 'dev'), parts along dimension 0
The draws below stay inside these ranges and needn't reach their ends.
There are 2 independent parts, one for each index of `stream`. The reference program is written for one: setup_inputs(seed, part) draws one part's arguments, and reference() takes and returns one part's arrays. A program takes and returns all parts, laid end to end along the dimension named above; an argument that names none is the same for every part. Nothing has to cross between parts.
Inputs may be any that keep to these rules, and one draw needn't show every extreme that they name: `owners`: each entry is the index of a device on dev.
All inputs are finite; a program needn't handle non-finite values.
Results may differ from the reference program's by a relative error of at most 0.0052.
Values may be sent and summed in bfloat16 or wider, within the bound.
No kernel may reach another device: no remote copies, remote signals or barrier semaphores. Data moves between devices by JAX's collectives and lax.ppermute only.
A program may use at most 128 MiB of HBM per device.

```python
import jax
import jax.numpy as jnp
from jax import lax

ZC = 16
CH = 384
GROUPS = 2
FRAMES = 3
COLS = 104
H = 16
N_DEV = 16


def block_levels(own_key, extent, shards, smallest, largest):
    def one(position, shards_of):
        steps = jax.random.uniform(jax.random.fold_in(jax.random.fold_in(own_key, 6), position), (shards_of,), jnp.float32, smallest / len(shards), largest / len(shards))
        return jnp.repeat(jnp.exp(steps), extent[position] // shards_of).reshape((-1,) + (1,) * (len(extent) - position - 1))

    gain = one(*shards[0])
    for cut in shards[1:]:
        gain = gain * one(*cut)
    return gain


def gaussian(own_key, extent, scale, most, pieces=(), kind=jnp.bfloat16):
    array = jax.random.normal(own_key, extent, jnp.float32) * scale
    if len(pieces) > 0:
        array = block_levels(own_key, extent, pieces, -0.22, 0.18) * array
    return jnp.clip(array, min=-most, max=most).astype(kind)


def setup_inputs(seed: int = 0, part: int = 0) -> dict:
    key_of = jax.random.split(jax.random.key(seed), 6)
    own_keys = jax.random.split(jax.random.fold_in(key_of[5], part), 6)
    latents = gaussian(own_keys[0], (N_DEV, GROUPS, FRAMES, H, COLS * ZC), 1.0, 6.0, ((0, 16),))
    owners = jax.random.randint(own_keys[1], (GROUPS,), 0, N_DEV).astype(jnp.int32)
    conv_in = gaussian(key_of[2], (27 * ZC, CH), (27 * ZC) ** -0.5, 0.3125)
    conv_mid = gaussian(key_of[3], (27 * CH, CH), (27 * CH) ** -0.5, 0.0625)
    to_pixels = gaussian(key_of[4], (CH, 12), CH ** -0.5, 0.3125)
    return dict(latents=latents, owners=owners, conv_in=conv_in, conv_mid=conv_mid, to_pixels=to_pixels)


epsilon = 1e-06

def causal_conv(source, weights, channels):
    padded = jnp.pad(source, ((2, 0), (1, 1), (1, 1), (0, 0)))
    steps_t = source.shape[0]
    rows_all = source.shape[1]
    columns = source.shape[2]
    accum_sum = jnp.zeros((steps_t * rows_all * columns, weights.shape[1]), jnp.float32)
    tap_index = 0
    for step_t in range(3):
        for step_r in range(3):
            for step_w in range(3):
                piece = padded[step_t:step_t + steps_t, step_r:step_r + rows_all, step_w:step_w + columns]
                block = weights[tap_index * channels:(tap_index + 1) * channels]
                accum_sum = accum_sum + jnp.dot(piece.reshape(-1, channels), block, preferred_element_type=jnp.float32)
                tap_index += 1
    return accum_sum.reshape(steps_t, rows_all, columns, weights.shape[1])

def rms_scale(values):
    return values * lax.rsqrt(lax.optimization_barrier(jnp.mean(values * values, axis=-1, keepdims=True)) + epsilon)

def reference(latents, owners, conv_in, conv_mid, to_pixels):
    picked = latents[owners, jnp.arange(GROUPS, dtype=jnp.int32)]
    frames = picked.reshape(GROUPS * FRAMES, H, COLS, ZC)
    first_act = causal_conv(frames, conv_in, ZC)
    activated = jax.nn.silu(rms_scale(first_act)).astype(jnp.bfloat16)
    second_act = causal_conv(activated, conv_mid, CH)
    normed = rms_scale(first_act + second_act).astype(jnp.bfloat16)
    projected = jnp.dot(normed.reshape(-1, CH), to_pixels, preferred_element_type=jnp.float32)
    projected = projected.reshape(GROUPS * FRAMES, H, COLS, 2, 2, 3)
    projected = projected.transpose(0, 1, 3, 2, 4, 5)
    return projected.reshape(GROUPS, FRAMES, 2 * H, 6 * COLS).astype(jnp.bfloat16)
```

```python
import jax
import jax.numpy as jnp
from jax import lax
from jax.sharding import PartitionSpec as P

ZC = 16
HALO = 2

epsilon = 1e-06

DIMS = ("NDHWC", "DHWIO", "NDHWC")


def rms_scale(values):
    return values * lax.rsqrt(jnp.mean(values * values, axis=-1, keepdims=True) + epsilon)


def gather_rows(x, n, rows_dev, position):
    bits = n.bit_length() - 1
    for k in reversed(range(bits)):
        half = (1 << k) * rows_dev
        size = half + 2 * HALO
        bit = (position >> k) & 1
        own = lax.dynamic_slice_in_dim(x, bit * half, size, 0)
        send = lax.dynamic_slice_in_dim(x, (1 - bit) * half, size, 0)
        pairs = [(i, i ^ (1 << k)) for i in range(n)]
        x = own + lax.ppermute(send, "dev", pairs)
    return x


def causal_conv(source, weights, channels):
    padded = jnp.pad(source, ((2, 0), (0, 0), (1, 1), (0, 0)))
    kernel = weights.reshape(3, 3, 3, channels, weights.shape[1])
    out = lax.conv_general_dilated(
        padded[None],
        kernel,
        window_strides=(1, 1, 1),
        padding="VALID",
        dimension_numbers=DIMS,
        preferred_element_type=jnp.float32,
    )
    return out[0]


def local(latents, owners, conv_in, conv_mid, to_pixels):
    n = lax.axis_size("dev")
    assert n & (n - 1) == 0
    position = lax.axis_index("dev")
    groups, frames, height, width = latents.shape[1:]
    columns = width // ZC
    channels = conv_mid.shape[1]
    rows_dev = height // n

    x = jnp.transpose(latents[0], (2, 0, 1, 3))
    keep = owners == position
    x = jnp.where(keep[None, :, None, None], x, jnp.zeros_like(x))
    x = jnp.pad(x, ((HALO, HALO), (0, 0), (0, 0), (0, 0)))
    x = gather_rows(x, n, rows_dev, position)

    window = jnp.transpose(x, (1, 2, 0, 3)).reshape(groups * frames, rows_dev + 2 * HALO, columns, ZC)
    first_act = causal_conv(window, conv_in, ZC)
    activated = jax.nn.silu(rms_scale(first_act)).astype(jnp.bfloat16)
    row_of = position * rows_dev - 1 + jnp.arange(rows_dev + 2)
    inside = (row_of >= 0) & (row_of < height)
    activated = jnp.where(inside[None, :, None, None], activated, jnp.zeros_like(activated))
    second_act = causal_conv(activated, conv_mid, channels)
    summed = first_act[:, 1 : 1 + rows_dev] + second_act
    normed = rms_scale(summed).astype(jnp.bfloat16)
    projected = jnp.dot(normed.reshape(-1, channels), to_pixels, preferred_element_type=jnp.float32)
    projected = projected.reshape(groups, frames, rows_dev, columns, 2, 2, 3).transpose(0, 1, 2, 4, 3, 5, 6)
    return projected.reshape(groups, frames, 2 * rows_dev, 6 * columns).astype(jnp.bfloat16)


def solution(mesh):
    in_specs = (P(("stream", "dev"), None, None, None, None), P("stream"), P(), P(), P())
    out_specs = P("stream", None, "dev", None)
    return jax.shard_map(local, mesh=mesh, in_specs=in_specs, out_specs=out_specs, check_vma=False)
```

```python
import jax
import jax.numpy as jnp
from jax import lax
from jax.sharding import PartitionSpec as P

ZC = 16
HALO = 2

epsilon = 1e-06

DIMS = ("NDHWC", "DHWIO", "NDHWC")


def rms_scale(values):
    return values * lax.rsqrt(jnp.mean(values * values, axis=-1, keepdims=True) + epsilon)


def reverse_bits(value, bits):
    return sum(((value >> b) & 1) << (bits - 1 - b) for b in range(bits))


def gather_rows(x, n, rows_dev, slot):
    bits = n.bit_length() - 1
    for k in reversed(range(bits)):
        half = (1 << k) * rows_dev
        size = half + 2 * HALO
        bit = (slot >> k) & 1
        own = lax.dynamic_slice_in_dim(x, bit * half, size, 0)
        send = lax.dynamic_slice_in_dim(x, (1 - bit) * half, size, 0)
        flip = 1 << (bits - 1 - k)
        pairs = [(i, i ^ flip) for i in range(n)]
        x = own + lax.ppermute(send, "dev", pairs)
    return x


def causal_conv(source, weights, channels):
    padded = jnp.pad(source, ((2, 0), (0, 0), (1, 1), (0, 0)))
    kernel = weights.reshape(3, 3, 3, channels, weights.shape[1])
    out = lax.conv_general_dilated(
        padded[None],
        kernel,
        window_strides=(1, 1, 1),
        padding="VALID",
        dimension_numbers=DIMS,
        preferred_element_type=jnp.float32,
    )
    return out[0]


def local(latents, owners, conv_in, conv_mid, to_pixels):
    n = lax.axis_size("dev")
    assert n & (n - 1) == 0
    position = lax.axis_index("dev")
    groups, frames, height, width = latents.shape[1:]
    columns = width // ZC
    channels = conv_mid.shape[1]
    rows_dev = height // n
    bits = n.bit_length() - 1
    slot = reverse_bits(position, bits)

    x = jnp.transpose(latents[0], (2, 0, 1, 3))
    keep = owners == position
    x = jnp.where(keep[None, :, None, None], x, jnp.zeros_like(x))
    x = jnp.pad(x, ((HALO, HALO), (0, 0), (0, 0), (0, 0)))
    x = gather_rows(x, n, rows_dev, slot)

    window = jnp.transpose(x, (1, 2, 0, 3)).reshape(groups * frames, rows_dev + 2 * HALO, columns, ZC)
    first_act = causal_conv(window, conv_in, ZC)
    activated = jax.nn.silu(rms_scale(first_act)).astype(jnp.bfloat16)
    row_of = slot * rows_dev - 1 + jnp.arange(rows_dev + 2)
    inside = (row_of >= 0) & (row_of < height)
    activated = jnp.where(inside[None, :, None, None], activated, jnp.zeros_like(activated))
    second_act = causal_conv(activated, conv_mid, channels)
    summed = first_act[:, 1 : 1 + rows_dev] + second_act
    normed = rms_scale(summed).astype(jnp.bfloat16)
    projected = jnp.dot(normed.reshape(-1, channels), to_pixels, preferred_element_type=jnp.float32)
    projected = projected.reshape(groups, frames, rows_dev, columns, 2, 2, 3).transpose(0, 1, 2, 4, 3, 5, 6)
    pixels = projected.reshape(groups, frames, 2 * rows_dev, 6 * columns).astype(jnp.bfloat16)
    return lax.ppermute(pixels, "dev", [(i, reverse_bits(i, bits)) for i in range(n)])


def solution(mesh):
    in_specs = (P(("stream", "dev"), None, None, None, None), P("stream"), P(), P(), P())
    out_specs = P("stream", None, "dev", None)
    return jax.shard_map(local, mesh=mesh, in_specs=in_specs, out_specs=out_specs, check_vma=False)
```

```python
import jax
import jax.numpy as jnp
from jax import lax
from jax.sharding import PartitionSpec as P

ZC = 16
HALO = 2

epsilon = 1e-06

DIMS = ("NDHWC", "DHWIO", "NDHWC")


def rms_scale(values):
    return values * lax.rsqrt(jnp.mean(values * values, axis=-1, keepdims=True) + epsilon)


def reverse_bits(value, bits):
    return sum(((value >> b) & 1) << (bits - 1 - b) for b in range(bits))


def gather_rows(x, n, rows_dev, slot, hooks=()):
    bits = n.bit_length() - 1
    for k in reversed(range(bits)):
        half = (1 << k) * rows_dev
        size = half + 2 * HALO
        bit = (slot >> k) & 1
        own = lax.dynamic_slice_in_dim(x, bit * half, size, 0)
        send = lax.dynamic_slice_in_dim(x, (1 - bit) * half, size, 0)
        flip = 1 << (bits - 1 - k)
        pairs = [(i, i ^ flip) for i in range(n)]
        x = own + lax.ppermute(send, "dev", pairs)
        step = bits - 1 - k
        if step < len(hooks):
            x = hooks[step](x)
    return x


def causal_conv(source, history, weights, channels):
    padded = jnp.pad(jnp.concatenate([history, source], axis=0), ((0, 0), (0, 0), (1, 1), (0, 0)))
    kernel = weights.reshape(3, 3, 3, channels, weights.shape[1])
    out = lax.conv_general_dilated(
        padded[None],
        kernel,
        window_strides=(1, 1, 1),
        padding="VALID",
        dimension_numbers=DIMS,
        preferred_element_type=jnp.float32,
    )
    return out[0]


def local(latents, owners, conv_in, conv_mid, to_pixels):
    n = lax.axis_size("dev")
    assert n & (n - 1) == 0
    position = lax.axis_index("dev")
    groups, frames, height, width = latents.shape[1:]
    columns = width // ZC
    channels = conv_mid.shape[1]
    rows_dev = height // n
    bits = n.bit_length() - 1
    slot = reverse_bits(position, bits)
    row_of = slot * rows_dev - 1 + jnp.arange(rows_dev + 2)
    inside = (row_of >= 0) & (row_of < height)

    def prepare(group):
        x = jnp.transpose(latents[0, group], (1, 0, 2))
        x = jnp.where(owners[group] == position, x, jnp.zeros_like(x))
        return jnp.pad(x, ((HALO, HALO), (0, 0), (0, 0)))

    def to_window(x):
        return jnp.transpose(x, (1, 0, 2)).reshape(frames, rows_dev + 2 * HALO, columns, ZC)

    def stages(state):
        def first(st):
            st["first"] = causal_conv(st["window"], st["x_history"], conv_in, ZC)

        def activate(st):
            activated = jax.nn.silu(rms_scale(st["first"])).astype(jnp.bfloat16)
            st["activated"] = jnp.where(inside[None, :, None, None], activated, jnp.zeros_like(activated))

        def second(st):
            st["second"] = causal_conv(st["activated"], st["a_history"], conv_mid, channels)

        def finish(st):
            summed = st["first"][:, 1 : 1 + rows_dev] + st["second"]
            normed = rms_scale(summed).astype(jnp.bfloat16)
            projected = jnp.dot(normed.reshape(-1, channels), to_pixels, preferred_element_type=jnp.float32)
            projected = projected.reshape(frames, rows_dev, columns, 2, 2, 3).transpose(0, 1, 3, 2, 4, 5)
            st["pixels"] = projected.reshape(frames, 2 * rows_dev, 6 * columns).astype(jnp.bfloat16)

        return [first, activate, second, finish]

    x_history = jnp.zeros((2, rows_dev + 2 * HALO, columns, ZC), jnp.bfloat16)
    a_history = jnp.zeros((2, rows_dev + 2, columns, channels), jnp.bfloat16)
    window = to_window(gather_rows(prepare(0), n, rows_dev, slot))
    results = []
    for group in range(groups):
        state = {"window": window, "x_history": x_history, "a_history": a_history}
        steps = stages(state)
        if group + 1 < groups:
            def hook_for(run):
                def hook(x):
                    run(state)
                    keys = sorted(state)
                    x, values = lax.optimization_barrier((x, [state[k] for k in keys]))
                    state.update(zip(keys, values))
                    return x

                return hook

            nxt = prepare(group + 1)
            nxt, window = lax.optimization_barrier((nxt, window))
            state["window"] = window
            hooks = [hook_for(run) for run in steps[: bits - 1]]
            nxt = gather_rows(nxt, n, rows_dev, slot, hooks)
            for run in steps[bits - 1 :]:
                run(state)
            next_window = to_window(nxt)
        else:
            for run in steps:
                run(state)
        results.append(state["pixels"])
        x_history = jnp.concatenate([x_history, state["window"]], axis=0)[-2:]
        a_history = jnp.concatenate([a_history, state["activated"]], axis=0)[-2:]
        if group + 1 < groups:
            window = next_window
    pixels = jnp.stack(results, axis=0)
    return lax.ppermute(pixels, "dev", [(i, reverse_bits(i, bits)) for i in range(n)])


def solution(mesh):
    in_specs = (P(("stream", "dev"), None, None, None, None), P("stream"), P(), P(), P())
    out_specs = P("stream", None, "dev", None)
    return jax.shard_map(local, mesh=mesh, in_specs=in_specs, out_specs=out_specs, check_vma=False)
```

```python
import jax
import jax.numpy as jnp
from jax import lax
from jax.sharding import PartitionSpec as P

ZC = 16
HALO = 2

epsilon = 1e-06

DIMS = ("NDHWC", "DHWIO", "NDHWC")


def rms_scale(values):
    return values * lax.rsqrt(jnp.mean(values * values, axis=-1, keepdims=True) + epsilon)


def reverse_bits(value, bits):
    return sum(((value >> b) & 1) << (bits - 1 - b) for b in range(bits))


def gather_rows(x, n, rows_dev, slot):
    bits = n.bit_length() - 1
    for k in reversed(range(bits)):
        half = (1 << k) * rows_dev
        size = half + 2 * HALO
        bit = (slot >> k) & 1
        own = lax.dynamic_slice_in_dim(x, bit * half, size, 0)
        send = lax.dynamic_slice_in_dim(x, (1 - bit) * half, size, 0)
        flip = 1 << (bits - 1 - k)
        pairs = [(i, i ^ flip) for i in range(n)]
        x = own + lax.ppermute(send, "dev", pairs)
    return x


def causal_conv(source, weights, channels):
    padded = jnp.pad(source, ((2, 0), (0, 0), (1, 1), (0, 0)))
    kernel = weights.reshape(3, 3, 3, channels, weights.shape[1])
    out = lax.conv_general_dilated(
        padded[None],
        kernel,
        window_strides=(1, 1, 1),
        padding="VALID",
        dimension_numbers=DIMS,
        preferred_element_type=jnp.float32,
    )
    return out[0]


def local(latents, owners, conv_in, conv_mid, to_pixels):
    n = lax.axis_size("dev")
    assert n & (n - 1) == 0
    position = lax.axis_index("dev")
    groups, frames, height, width = latents.shape[1:]
    columns = width // ZC
    channels = conv_mid.shape[1]
    rows_dev = height // n
    bits = n.bit_length() - 1
    slot = reverse_bits(position, bits)

    x = jnp.transpose(latents[0], (2, 0, 1, 3))
    keep = owners == position
    x = jnp.where(keep[None, :, None, None], x, jnp.zeros_like(x))
    x = jnp.pad(x, ((HALO, HALO), (0, 0), (0, 0), (0, 0)))
    x = gather_rows(x, n, rows_dev, slot)

    window = jnp.transpose(x, (1, 2, 0, 3)).reshape(groups * frames, rows_dev + 2 * HALO, columns, ZC)
    steps = groups * frames
    rows_in = rows_dev + 2
    padded = jnp.pad(window, ((2, 0), (0, 0), (1, 1), (0, 0)))
    pieces = [
        padded[a : a + steps, b : b + rows_in, e : e + columns]
        for a in range(3)
        for b in range(3)
        for e in range(3)
    ]
    xcol = jnp.concatenate(pieces, axis=-1).reshape(-1, 27 * ZC)
    first_act = jnp.dot(xcol, conv_in, preferred_element_type=jnp.float32)
    first_act = first_act.reshape(steps, rows_in, columns, channels)
    activated = jax.nn.silu(rms_scale(first_act)).astype(jnp.bfloat16)
    row_of = slot * rows_dev - 1 + jnp.arange(rows_dev + 2)
    inside = (row_of >= 0) & (row_of < height)
    activated = jnp.where(inside[None, :, None, None], activated, jnp.zeros_like(activated))
    second_act = causal_conv(activated, conv_mid, channels)
    summed = first_act[:, 1 : 1 + rows_dev] + second_act
    normed = rms_scale(summed).astype(jnp.bfloat16)
    projected = jnp.dot(normed.reshape(-1, channels), to_pixels, preferred_element_type=jnp.float32)
    projected = projected.reshape(groups, frames, rows_dev, columns, 2, 2, 3).transpose(0, 1, 2, 4, 3, 5, 6)
    pixels = projected.reshape(groups, frames, 2 * rows_dev, 6 * columns).astype(jnp.bfloat16)
    return lax.ppermute(pixels, "dev", [(i, reverse_bits(i, bits)) for i in range(n)])


def solution(mesh):
    in_specs = (P(("stream", "dev"), None, None, None, None), P("stream"), P(), P(), P())
    out_specs = P("stream", None, "dev", None)
    return jax.shard_map(local, mesh=mesh, in_specs=in_specs, out_specs=out_specs, check_vma=False)
```

```python
import jax
import jax.numpy as jnp
from jax import lax
from jax.experimental import pallas as pl
from jax.experimental.pallas import tpu as pltpu
from jax.sharding import PartitionSpec as P

ZC = 16
HALO = 2

epsilon = 1e-06

def rms_scale(values):
    return values * lax.rsqrt(jnp.mean(values * values, axis=-1, keepdims=True) + epsilon)


def reverse_bits(value, bits):
    return sum(((value >> b) & 1) << (bits - 1 - b) for b in range(bits))


def gather_rows(x, n, rows_dev, slot):
    bits = n.bit_length() - 1
    for k in reversed(range(bits)):
        half = (1 << k) * rows_dev
        size = half + 2 * HALO
        bit = (slot >> k) & 1
        own = lax.dynamic_slice_in_dim(x, bit * half, size, 0)
        send = lax.dynamic_slice_in_dim(x, (1 - bit) * half, size, 0)
        flip = 1 << (bits - 1 - k)
        pairs = [(i, i ^ flip) for i in range(n)]
        x = own + lax.ppermute(send, "dev", pairs)
    return x


def decode_kernel(row_ok_ref, xcol_ref, w_in_ref, w_vmem, w_pix_ref, out_ref, act_ref, center_ref):
    rows_in, span, _ = xcol_ref.shape
    rows_out = rows_in - 2
    lead = act_ref.shape[2] - span
    cp = lead // 2
    channels = act_ref.shape[3]
    taps = w_vmem.shape[0] // 3
    zeros = jnp.zeros((lead, channels), act_ref.dtype)
    for e in range(3):
        for j in range(rows_in):
            act_ref[e, j, 0:lead, :] = zeros
    w_in = w_in_ref[...]
    for j in range(rows_in):
        first = jnp.dot(xcol_ref[j], w_in, preferred_element_type=jnp.float32)
        if 1 <= j <= rows_out:
            center_ref[j - 1] = first
        scaled = first * lax.rsqrt(jnp.mean(first * first, axis=-1, keepdims=True) + epsilon)
        act = scaled / (1.0 + jnp.exp(-scaled)) * row_ok_ref[j]
        act_ref[1, j, lead:, :] = act.astype(act_ref.dtype)
        act_ref[0, j, lead:, :] = pltpu.roll(act, 1, 0).astype(act_ref.dtype)
        act_ref[2, j, lead:, :] = pltpu.roll(act, span - 1, 0).astype(act_ref.dtype)
    for jo in range(rows_out):

        def tap(t, acc):
            a = t // 9
            b = (t // 3) % 3
            e = t % 3
            start = pl.multiple_of(a * cp, 16)
            piece = act_ref[e, jo + b, pl.ds(start, span), :]
            return acc + jnp.dot(piece, w_vmem[t], preferred_element_type=jnp.float32)

        acc = lax.fori_loop(0, 27, tap, center_ref[jo])
        scale = lax.rsqrt(jnp.mean(acc * acc, axis=-1, keepdims=True) + epsilon)
        normed = (acc * scale).astype(jnp.bfloat16)
        out_ref[jo] = jnp.dot(normed, w_pix_ref[...], preferred_element_type=jnp.float32)


def decode(row_ok, xcol, conv_in, conv_mid, to_pixels, cp):
    rows_in, span, _ = xcol.shape
    channels = conv_mid.shape[1]
    w_mid = conv_mid.reshape(27, channels, channels)
    lanes = 128
    k_in = -(-xcol.shape[2] // lanes) * lanes
    xcol = jnp.pad(xcol, ((0, 0), (0, 0), (0, k_in - xcol.shape[2])))
    conv_in = jnp.pad(conv_in, ((0, k_in - conv_in.shape[0]), (0, 0)))
    n_pix = to_pixels.shape[1]
    to_pixels = jnp.pad(to_pixels, ((0, 0), (0, lanes - n_pix)))
    vmem = pltpu.MemorySpace.VMEM
    return pl.pallas_call(
        decode_kernel,
        out_shape=jax.ShapeDtypeStruct((rows_in - 2, span, lanes), jnp.float32),
        in_specs=[
            pl.BlockSpec(memory_space=pltpu.MemorySpace.SMEM),
            pl.BlockSpec(memory_space=vmem),
            pl.BlockSpec(memory_space=vmem),
            pl.BlockSpec(memory_space=vmem),
            pl.BlockSpec(memory_space=vmem),
        ],
        out_specs=pl.BlockSpec(memory_space=vmem),
        scratch_shapes=[
            pltpu.VMEM((3, rows_in, span + 2 * cp, channels), jnp.bfloat16),
            pltpu.VMEM((rows_in - 2, span, channels), jnp.float32),
        ],
        compiler_params=pltpu.CompilerParams(vmem_limit_bytes=48 * 1024 * 1024),
    )(row_ok, xcol, conv_in, w_mid, to_pixels)[:, :, :n_pix]


def local(latents, owners, conv_in, conv_mid, to_pixels):
    n = lax.axis_size("dev")
    assert n & (n - 1) == 0
    position = lax.axis_index("dev")
    groups, frames, height, width = latents.shape[1:]
    columns = width // ZC
    rows_dev = height // n
    bits = n.bit_length() - 1
    slot = reverse_bits(position, bits)
    cp = -(-columns // 16) * 16
    steps = groups * frames

    x = jnp.transpose(latents[0], (2, 0, 1, 3))
    keep = owners == position
    x = jnp.where(keep[None, :, None, None], x, jnp.zeros_like(x))
    x = jnp.pad(x, ((HALO, HALO), (0, 0), (0, 0), (0, 0)))
    x = gather_rows(x, n, rows_dev, slot)

    rows_in = rows_dev + 2
    window = jnp.transpose(x, (1, 2, 0, 3)).reshape(steps, rows_dev + 2 * HALO, columns, ZC)
    padded = jnp.pad(window, ((2, 0), (0, 0), (1, 1 + cp - columns), (0, 0)))
    pieces = [
        padded[a : a + steps, b : b + rows_in, e : e + cp]
        for a in range(3)
        for b in range(3)
        for e in range(3)
    ]
    xcol = jnp.concatenate(pieces, axis=-1)
    col_ok = jnp.arange(cp) < columns
    xcol = jnp.where(col_ok[None, None, :, None], xcol, jnp.zeros_like(xcol))
    xcol = jnp.transpose(xcol, (1, 0, 2, 3)).reshape(rows_in, steps * cp, 27 * ZC)
    row_of = slot * rows_dev - 1 + jnp.arange(rows_in)
    row_ok = ((row_of >= 0) & (row_of < height)).astype(jnp.float32)

    projected = decode(row_ok, xcol, conv_in, conv_mid, to_pixels, cp)
    projected = projected.reshape(rows_dev, groups, frames, cp, 2, 2, 3)[:, :, :, :columns]
    projected = projected.transpose(1, 2, 0, 4, 3, 5, 6)
    pixels = projected.reshape(groups, frames, 2 * rows_dev, 6 * columns).astype(jnp.bfloat16)
    return lax.ppermute(pixels, "dev", [(i, reverse_bits(i, bits)) for i in range(n)])


def solution(mesh):
    in_specs = (P(("stream", "dev"), None, None, None, None), P("stream"), P(), P(), P())
    out_specs = P("stream", None, "dev", None)
    return jax.shard_map(local, mesh=mesh, in_specs=in_specs, out_specs=out_specs, check_vma=False)
```

```python
import jax
import jax.numpy as jnp
from jax import lax
from jax.sharding import PartitionSpec as P

ZC = 16
HALO = 2

epsilon = 1e-06

DIMS = ("NDHWC", "DHWIO", "NDHWC")


def rms_scale(values):
    return values * lax.rsqrt(jnp.mean(values * values, axis=-1, keepdims=True) + epsilon)


def reverse_bits(value, bits):
    return sum(((value >> b) & 1) << (bits - 1 - b) for b in range(bits))


def gather_rows(x, n, rows_dev, slot):
    bits = n.bit_length() - 1
    for k in reversed(range(bits)):
        half = (1 << k) * rows_dev
        size = half + 2 * HALO
        bit = (slot >> k) & 1
        own = lax.dynamic_slice_in_dim(x, bit * half, size, 0)
        send = lax.dynamic_slice_in_dim(x, (1 - bit) * half, size, 0)
        flip = 1 << (bits - 1 - k)
        pairs = [(i, i ^ flip) for i in range(n)]
        x = own + lax.ppermute(send, "dev", pairs)
    return x


def causal_conv(source, weights, channels):
    padded = jnp.pad(source, ((2, 0), (0, 0), (1, 1), (0, 0)))
    kernel = weights.reshape(3, 3, 3, channels, weights.shape[1])
    out = lax.conv_general_dilated(
        padded[None],
        kernel,
        window_strides=(1, 1, 1),
        padding="VALID",
        dimension_numbers=DIMS,
        preferred_element_type=jnp.float32,
    )
    return out[0]


def local(latents, owners, conv_in, conv_mid, to_pixels):
    n = lax.axis_size("dev")
    assert n & (n - 1) == 0
    position = lax.axis_index("dev")
    groups, frames, height, width = latents.shape[1:]
    columns = width // ZC
    channels = conv_mid.shape[1]
    rows_dev = height // n
    bits = n.bit_length() - 1
    slot = reverse_bits(position, bits)

    x = jnp.transpose(latents[0], (2, 0, 1, 3))
    keep = owners == position
    x = jnp.where(keep[None, :, None, None], x, jnp.zeros_like(x))
    x = jnp.pad(x, ((HALO, HALO), (0, 0), (0, 0), (0, 0)))
    x = gather_rows(x, n, rows_dev, slot)

    window = jnp.transpose(x, (1, 2, 0, 3)).reshape(groups * frames, rows_dev + 2 * HALO, columns, ZC)
    steps = groups * frames
    framed = jnp.pad(window, ((2, 0), (0, 0), (1, 1), (0, 0)))
    stacked = jnp.concatenate([framed[a : a + steps] for a in range(3)], axis=-1)
    kernel_in = conv_in.reshape(3, 3, 3, ZC, channels).transpose(1, 2, 0, 3, 4).reshape(3, 3, 3 * ZC, channels)
    first_act = lax.conv_general_dilated(
        stacked,
        kernel_in,
        window_strides=(1, 1),
        padding="VALID",
        dimension_numbers=("NHWC", "HWIO", "NHWC"),
        preferred_element_type=jnp.float32,
    )
    activated = jax.nn.silu(rms_scale(first_act)).astype(jnp.bfloat16)
    row_of = slot * rows_dev - 1 + jnp.arange(rows_dev + 2)
    inside = (row_of >= 0) & (row_of < height)
    activated = jnp.where(inside[None, :, None, None], activated, jnp.zeros_like(activated))
    second_act = causal_conv(activated, conv_mid, channels)
    summed = first_act[:, 1 : 1 + rows_dev] + second_act
    normed = rms_scale(summed).astype(jnp.bfloat16)
    projected = jnp.dot(normed.reshape(-1, channels), to_pixels, preferred_element_type=jnp.float32)
    projected = projected.reshape(groups, frames, rows_dev, columns, 2, 2, 3).transpose(0, 1, 2, 4, 3, 5, 6)
    pixels = projected.reshape(groups, frames, 2 * rows_dev, 6 * columns).astype(jnp.bfloat16)
    return lax.ppermute(pixels, "dev", [(i, reverse_bits(i, bits)) for i in range(n)])


def solution(mesh):
    in_specs = (P(("stream", "dev"), None, None, None, None), P("stream"), P(), P(), P())
    out_specs = P("stream", None, "dev", None)
    return jax.shard_map(local, mesh=mesh, in_specs=in_specs, out_specs=out_specs, check_vma=False)
```

```python
import jax
import jax.numpy as jnp
from jax import lax
from jax.sharding import PartitionSpec as P

ZC = 16
HALO = 2

epsilon = 1e-06

DIMS = ("NDHWC", "DHWIO", "NDHWC")


def rms_scale(values):
    return values * lax.rsqrt(jnp.mean(values * values, axis=-1, keepdims=True) + epsilon)


def reverse_bits(value, bits):
    return sum(((value >> b) & 1) << (bits - 1 - b) for b in range(bits))


def gather_rows(x, n, rows_dev, slot):
    bits = n.bit_length() - 1
    for k in reversed(range(bits)):
        half = (1 << k) * rows_dev
        size = half + 2 * HALO
        bit = (slot >> k) & 1
        own = lax.dynamic_slice_in_dim(x, bit * half, size, 0)
        send = lax.dynamic_slice_in_dim(x, (1 - bit) * half, size, 0)
        flip = 1 << (bits - 1 - k)
        pairs = [(i, i ^ flip) for i in range(n)]
        x = own + lax.ppermute(send, "dev", pairs)
    return x


def causal_conv(source, weights, channels):
    padded = jnp.pad(source, ((2, 0), (0, 0), (1, 1), (0, 0)))
    kernel = weights.reshape(3, 3, 3, channels, weights.shape[1])
    out = lax.conv_general_dilated(
        padded[None],
        kernel,
        window_strides=(1, 1, 1),
        padding="VALID",
        dimension_numbers=DIMS,
        preferred_element_type=jnp.float32,
    )
    return out[0]


def local(latents, owners, conv_in, conv_mid, to_pixels):
    n = lax.axis_size("dev")
    assert n & (n - 1) == 0
    position = lax.axis_index("dev")
    groups, frames, height, width = latents.shape[1:]
    columns = width // ZC
    channels = conv_mid.shape[1]
    rows_dev = height // n
    bits = n.bit_length() - 1
    slot = reverse_bits(position, bits)

    x = jnp.transpose(latents[0], (2, 0, 1, 3))
    keep = owners == position
    x = jnp.where(keep[None, :, None, None], x, jnp.zeros_like(x))
    x = jnp.pad(x, ((HALO, HALO), (0, 0), (0, 0), (0, 0)))
    x = gather_rows(x, n, rows_dev, slot)

    steps = groups * frames
    rows_in = rows_dev + 2
    window = x.reshape(rows_dev + 2 * HALO, steps, columns, ZC).transpose(1, 0, 3, 2)
    window = jnp.pad(window, ((2, 0), (0, 0), (0, 0), (1, 1)))
    pieces = [
        window[a : a + steps, b : b + rows_in, :, e : e + columns]
        for a in range(3)
        for b in range(3)
        for e in range(3)
    ]
    xcol = jnp.concatenate(pieces, axis=2)
    first_cm = lax.dot_general(
        conv_in, xcol, (((0,), (2,)), ((), ())), preferred_element_type=jnp.float32
    )
    scale = lax.rsqrt(jnp.mean(first_cm * first_cm, axis=0, keepdims=True) + epsilon)
    activated = jax.nn.silu(first_cm * scale).astype(jnp.bfloat16)
    activated = jnp.transpose(activated, (1, 2, 3, 0))
    first_act = jnp.transpose(first_cm[:, :, 1 : 1 + rows_dev], (1, 2, 3, 0))
    row_of = slot * rows_dev - 1 + jnp.arange(rows_dev + 2)
    inside = (row_of >= 0) & (row_of < height)
    activated = jnp.where(inside[None, :, None, None], activated, jnp.zeros_like(activated))
    second_act = causal_conv(activated, conv_mid, channels)
    summed = first_act + second_act
    normed = rms_scale(summed).astype(jnp.bfloat16)
    projected = jnp.dot(normed.reshape(-1, channels), to_pixels, preferred_element_type=jnp.float32)
    projected = projected.reshape(groups, frames, rows_dev, columns, 2, 2, 3).transpose(0, 1, 2, 4, 3, 5, 6)
    pixels = projected.reshape(groups, frames, 2 * rows_dev, 6 * columns).astype(jnp.bfloat16)
    return lax.ppermute(pixels, "dev", [(i, reverse_bits(i, bits)) for i in range(n)])


def solution(mesh):
    in_specs = (P(("stream", "dev"), None, None, None, None), P("stream"), P(), P(), P())
    out_specs = P("stream", None, "dev", None)
    return jax.shard_map(local, mesh=mesh, in_specs=in_specs, out_specs=out_specs, check_vma=False)
```

```python
import jax
import jax.numpy as jnp
from jax import lax
from jax.sharding import PartitionSpec as P

ZC = 16
HALO = 2

epsilon = 1e-06

DIMS = ("NDHWC", "DHWIO", "NDHWC")


def rms_scale(values):
    return values * lax.rsqrt(jnp.mean(values * values, axis=-1, keepdims=True) + epsilon)


def scatter_rows(x, n, position):
    bits = n.bit_length() - 1
    for k in range(bits):
        bit = (position >> k) & 1
        split = x.reshape((x.shape[0] // 2, 2) + x.shape[1:])
        low, high = split[:, 0], split[:, 1]
        own = jnp.where(bit == 1, high, low)
        send = jnp.where(bit == 1, low, high)
        pairs = [(i, i ^ (1 << k)) for i in range(n)]
        x = own + lax.ppermute(send, "dev", pairs)
    return x[0]


def with_halo(block, n, halo):
    rows_dev = block.shape[0]
    reach = -(-halo // rows_dev)
    below, above = [], []
    for d in range(1, reach + 1):
        below.insert(0, lax.ppermute(block, "dev", [(i, i + d) for i in range(n - d)]))
        above.append(lax.ppermute(block, "dev", [(i + d, i) for i in range(n - d)]))
    joined = jnp.concatenate(below + [block] + above, axis=0)
    return joined[reach * rows_dev - halo : (reach + 1) * rows_dev + halo]


def causal_conv(source, weights, channels):
    padded = jnp.pad(source, ((2, 0), (0, 0), (1, 1), (0, 0)))
    kernel = weights.reshape(3, 3, 3, channels, weights.shape[1])
    out = lax.conv_general_dilated(
        padded[None],
        kernel,
        window_strides=(1, 1, 1),
        padding="VALID",
        dimension_numbers=DIMS,
        preferred_element_type=jnp.float32,
    )
    return out[0]


def local(latents, owners, conv_in, conv_mid, to_pixels):
    n = lax.axis_size("dev")
    assert n & (n - 1) == 0
    position = lax.axis_index("dev")
    groups, frames, height, width = latents.shape[1:]
    columns = width // ZC
    channels = conv_mid.shape[1]
    rows_dev = height // n
    x = jnp.transpose(latents[0], (2, 0, 1, 3))
    keep = owners == position
    x = jnp.where(keep[None, :, None, None], x, jnp.zeros_like(x))
    x = scatter_rows(x.reshape((n, rows_dev) + x.shape[1:]), n, position)
    x = with_halo(x, n, HALO)

    window = jnp.transpose(x, (1, 2, 0, 3)).reshape(groups * frames, rows_dev + 2 * HALO, columns, ZC)
    first_act = causal_conv(window, conv_in, ZC)
    activated = jax.nn.silu(rms_scale(first_act)).astype(jnp.bfloat16)
    row_of = position * rows_dev - 1 + jnp.arange(rows_dev + 2)
    inside = (row_of >= 0) & (row_of < height)
    activated = jnp.where(inside[None, :, None, None], activated, jnp.zeros_like(activated))
    second_act = causal_conv(activated, conv_mid, channels)
    summed = first_act[:, 1 : 1 + rows_dev] + second_act
    normed = rms_scale(summed).astype(jnp.bfloat16)
    projected = jnp.dot(normed.reshape(-1, channels), to_pixels, preferred_element_type=jnp.float32)
    projected = projected.reshape(groups, frames, rows_dev, columns, 2, 2, 3).transpose(0, 1, 2, 4, 3, 5, 6)
    pixels = projected.reshape(groups, frames, 2 * rows_dev, 6 * columns).astype(jnp.bfloat16)
    return pixels


def solution(mesh):
    in_specs = (P(("stream", "dev"), None, None, None, None), P("stream"), P(), P(), P())
    out_specs = P("stream", None, "dev", None)
    return jax.shard_map(local, mesh=mesh, in_specs=in_specs, out_specs=out_specs, check_vma=False)
```

```python
import functools

import jax
import jax.numpy as jnp
from jax import lax
from jax.experimental import pallas as pl
from jax.experimental.pallas import tpu as pltpu
from jax.sharding import PartitionSpec as P

ZC = 16
HALO = 2

epsilon = 1e-06

def rms_scale(values):
    return values * lax.rsqrt(jnp.mean(values * values, axis=-1, keepdims=True) + epsilon)


def reverse_bits(value, bits):
    return sum(((value >> b) & 1) << (bits - 1 - b) for b in range(bits))


def gather_rows(x, n, rows_dev, slot):
    bits = n.bit_length() - 1
    for k in reversed(range(bits)):
        half = (1 << k) * rows_dev
        size = half + 2 * HALO
        bit = (slot >> k) & 1
        own = lax.dynamic_slice_in_dim(x, bit * half, size, 0)
        send = lax.dynamic_slice_in_dim(x, (1 - bit) * half, size, 0)
        flip = 1 << (bits - 1 - k)
        pairs = [(i, i ^ flip) for i in range(n)]
        x = own + lax.ppermute(send, "dev", pairs)
    return x


LANE = 128


def decode_kernel(columns, row_ok_ref, xt_ref, w_in_ref, w_hbm, w_pix_ref, out_ref, w_vmem, act_ref, center_ref, sem):
    rows_in = act_ref.shape[1]
    rows_out = rows_in - 2
    lead = 2 * LANE
    span = act_ref.shape[2] - lead
    channels = act_ref.shape[3]
    taps = w_vmem.shape[0] // 3
    copies = [
        pltpu.make_async_copy(w_hbm.at[pl.ds(a * taps, taps)], w_vmem.at[pl.ds(a * taps, taps)], sem.at[a])
        for a in range(3)
    ]
    for copy in copies:
        copy.start()
    zeros = jnp.zeros((lead, channels), act_ref.dtype)
    for e in range(3):
        for j in range(rows_in):
            act_ref[e, j, 0:lead, :] = zeros
    column = lax.broadcasted_iota(jnp.int32, (span, 1), 0) % LANE
    valid = column < columns
    w_in = w_in_ref[...]
    for j in range(rows_in):
        pieces = []
        for a in range(3):
            for b in range(3):
                src = xt_ref[j + b, :, a * LANE : a * LANE + span].astype(jnp.float32)
                for e in range(3):
                    shifted = src if e == 1 else pltpu.roll(src, (1 - e) % span, 1)
                    pieces.append(shifted.astype(jnp.bfloat16))
        patches = jnp.concatenate(pieces, axis=0)
        first_t = jnp.dot(w_in, patches, preferred_element_type=jnp.float32)
        first = jnp.where(valid, first_t.T, 0.0)
        if 1 <= j <= rows_out:
            center_ref[j - 1] = first
        scaled = first * lax.rsqrt(jnp.mean(first * first, axis=-1, keepdims=True) + epsilon)
        act = scaled / (1.0 + jnp.exp(-scaled)) * row_ok_ref[j]
        act_ref[1, j, lead:, :] = act.astype(act_ref.dtype)
        act_ref[0, j, lead:, :] = pltpu.roll(act, 1, 0).astype(act_ref.dtype)
        act_ref[2, j, lead:, :] = pltpu.roll(act, span - 1, 0).astype(act_ref.dtype)
    for copy in copies:
        copy.wait()
    for jo in range(rows_out):

        def time_tap(a, acc):
            start = pl.multiple_of(a * LANE, LANE)
            for b in range(3):
                for e in range(3):
                    piece = act_ref[e, jo + b, pl.ds(start, span), :]
                    acc = acc + jnp.dot(piece, w_vmem[a * taps + b * 3 + e], preferred_element_type=jnp.float32)
            return acc

        acc = lax.fori_loop(0, 3, time_tap, center_ref[jo])
        scale = lax.rsqrt(jnp.mean(acc * acc, axis=-1, keepdims=True) + epsilon)
        normed = (acc * scale).astype(jnp.bfloat16)
        out_ref[jo] = jnp.dot(normed, w_pix_ref[...], preferred_element_type=jnp.float32)


def decode(row_ok, xt, conv_in, conv_mid, to_pixels, columns):
    rows_in = xt.shape[0] - 2
    span = xt.shape[2] - 2 * LANE
    channels = conv_mid.shape[1]
    w_mid = conv_mid.reshape(27, channels, channels)
    w_in_t = conv_in.T
    n_pix = to_pixels.shape[1]
    w_pix = jnp.pad(to_pixels, ((0, 0), (0, LANE - n_pix)))
    vmem = pltpu.MemorySpace.VMEM
    out = pl.pallas_call(
        functools.partial(decode_kernel, columns),
        out_shape=jax.ShapeDtypeStruct((rows_in - 2, span, LANE), jnp.float32),
        in_specs=[
            pl.BlockSpec(memory_space=pltpu.MemorySpace.SMEM),
            pl.BlockSpec(memory_space=vmem),
            pl.BlockSpec(memory_space=vmem),
            pl.BlockSpec(memory_space=pl.ANY),
            pl.BlockSpec(memory_space=vmem),
        ],
        out_specs=pl.BlockSpec(memory_space=vmem),
        scratch_shapes=[
            pltpu.VMEM((27, channels, channels), jnp.bfloat16),
            pltpu.VMEM((3, rows_in, span + 2 * LANE, channels), jnp.bfloat16),
            pltpu.VMEM((rows_in - 2, span, channels), jnp.float32),
            pltpu.SemaphoreType.DMA((3,)),
        ],
        compiler_params=pltpu.CompilerParams(vmem_limit_bytes=48 * 1024 * 1024),
    )(row_ok, xt, w_in_t, w_mid, w_pix)
    return out[:, :, :n_pix]


def local(latents, owners, conv_in, conv_mid, to_pixels):
    n = lax.axis_size("dev")
    assert n & (n - 1) == 0
    position = lax.axis_index("dev")
    groups, frames, height, width = latents.shape[1:]
    columns = width // ZC
    rows_dev = height // n
    bits = n.bit_length() - 1
    slot = reverse_bits(position, bits)
    steps = groups * frames
    assert columns < LANE

    x = jnp.transpose(latents[0], (2, 0, 1, 3))
    keep = owners == position
    x = jnp.where(keep[None, :, None, None], x, jnp.zeros_like(x))
    x = jnp.pad(x, ((HALO, HALO), (0, 0), (0, 0), (0, 0)))
    x = gather_rows(x, n, rows_dev, slot)

    rows_in = rows_dev + 2
    xt = x.reshape(rows_dev + 2 * HALO, steps, columns, ZC).transpose(0, 3, 1, 2)
    xt = jnp.pad(xt, ((0, 0), (0, 0), (2, 0), (0, LANE - columns)))
    xt = xt.reshape(rows_dev + 2 * HALO, ZC, (steps + 2) * LANE)
    row_of = slot * rows_dev - 1 + jnp.arange(rows_in)
    row_ok = ((row_of >= 0) & (row_of < height)).astype(jnp.float32)

    projected = decode(row_ok, xt, conv_in, conv_mid, to_pixels, columns)
    projected = projected.reshape(rows_dev, groups, frames, LANE, 2, 2, 3)[:, :, :, :columns]
    projected = projected.transpose(1, 2, 0, 4, 3, 5, 6)
    pixels = projected.reshape(groups, frames, 2 * rows_dev, 6 * columns).astype(jnp.bfloat16)
    return lax.ppermute(pixels, "dev", [(i, reverse_bits(i, bits)) for i in range(n)])


def solution(mesh):
    in_specs = (P(("stream", "dev"), None, None, None, None), P("stream"), P(), P(), P())
    out_specs = P("stream", None, "dev", None)
    return jax.shard_map(local, mesh=mesh, in_specs=in_specs, out_specs=out_specs, check_vma=False)
```

```python
import functools

import jax
import jax.numpy as jnp
from jax import lax
from jax.experimental import pallas as pl
from jax.experimental.pallas import tpu as pltpu
from jax.sharding import PartitionSpec as P

ZC = 16
HALO = 2

epsilon = 1e-06

def rms_scale(values):
    return values * lax.rsqrt(jnp.mean(values * values, axis=-1, keepdims=True) + epsilon)


def reverse_bits(value, bits):
    return sum(((value >> b) & 1) << (bits - 1 - b) for b in range(bits))


def gather_rows(x, n, rows_dev, slot):
    bits = n.bit_length() - 1
    for k in reversed(range(bits)):
        half = (1 << k) * rows_dev
        size = half + 2 * HALO
        bit = (slot >> k) & 1
        own = lax.dynamic_slice_in_dim(x, bit * half, size, 0)
        send = lax.dynamic_slice_in_dim(x, (1 - bit) * half, size, 0)
        flip = 1 << (bits - 1 - k)
        pairs = [(i, i ^ flip) for i in range(n)]
        x = own + lax.ppermute(send, "dev", pairs)
    return x


LANE = 128


def decode_kernel(columns, row_ok_ref, xt_ref, w_in_ref, w_hbm, w_pix_ref, out_ref, w_vmem, act_ref, center_ref, sem):
    rows_in = act_ref.shape[0]
    rows_out = rows_in - 2
    lead = 2 * LANE
    span = act_ref.shape[1] - lead
    channels = w_vmem.shape[2]
    taps = w_vmem.shape[0] // 3
    copies = [
        pltpu.make_async_copy(w_hbm.at[pl.ds(a * taps, taps)], w_vmem.at[pl.ds(a * taps, taps)], sem.at[a])
        for a in range(3)
    ]
    for copy in copies:
        copy.start()
    zeros = jnp.zeros((lead, 3 * channels), act_ref.dtype)
    for j in range(rows_in):
        act_ref[j, 0:lead, :] = zeros
    column = lax.broadcasted_iota(jnp.int32, (span, 1), 0) % LANE
    valid = column < columns
    w_in = w_in_ref[...]
    for j in range(rows_in):
        pieces = []
        for a in range(3):
            for b in range(3):
                src = xt_ref[j + b, :, a * LANE : a * LANE + span].astype(jnp.float32)
                for e in range(3):
                    shifted = src if e == 1 else pltpu.roll(src, (1 - e) % span, 1)
                    pieces.append(shifted.astype(jnp.bfloat16))
        patches = jnp.concatenate(pieces, axis=0)
        first_t = jnp.dot(w_in, patches, preferred_element_type=jnp.float32)
        first = jnp.where(valid, first_t.T, 0.0)
        if 1 <= j <= rows_out:
            center_ref[j - 1] = first
        scaled = first * lax.rsqrt(jnp.mean(first * first, axis=-1, keepdims=True) + epsilon)
        act = scaled / (1.0 + jnp.exp(-scaled)) * row_ok_ref[j]
        act_ref[j, lead:, 0:channels] = pltpu.roll(act, 1, 0).astype(act_ref.dtype)
        act_ref[j, lead:, channels : 2 * channels] = act.astype(act_ref.dtype)
        act_ref[j, lead:, 2 * channels :] = pltpu.roll(act, span - 1, 0).astype(act_ref.dtype)
    for copy in copies:
        copy.wait()
    for jo in range(rows_out):

        def time_tap(a, acc):
            start = pl.multiple_of(a * LANE, LANE)
            for b in range(3):
                piece = act_ref[jo + b, pl.ds(start, span), :]
                acc = acc + jnp.dot(piece, w_vmem[a * taps + b], preferred_element_type=jnp.float32)
            return acc

        acc = lax.fori_loop(0, 3, time_tap, center_ref[jo])
        scale = lax.rsqrt(jnp.mean(acc * acc, axis=-1, keepdims=True) + epsilon)
        normed = (acc * scale).astype(jnp.bfloat16)
        out_ref[jo] = jnp.dot(normed, w_pix_ref[...], preferred_element_type=jnp.float32)


def decode(row_ok, xt, conv_in, conv_mid, to_pixels, columns):
    rows_in = xt.shape[0] - 2
    span = xt.shape[2] - 2 * LANE
    channels = conv_mid.shape[1]
    w_mid = conv_mid.reshape(9, 3 * channels, channels)
    w_in_t = conv_in.T
    n_pix = to_pixels.shape[1]
    w_pix = jnp.pad(to_pixels, ((0, 0), (0, LANE - n_pix)))
    vmem = pltpu.MemorySpace.VMEM
    out = pl.pallas_call(
        functools.partial(decode_kernel, columns),
        out_shape=jax.ShapeDtypeStruct((rows_in - 2, span, LANE), jnp.float32),
        in_specs=[
            pl.BlockSpec(memory_space=pltpu.MemorySpace.SMEM),
            pl.BlockSpec(memory_space=vmem),
            pl.BlockSpec(memory_space=vmem),
            pl.BlockSpec(memory_space=pl.ANY),
            pl.BlockSpec(memory_space=vmem),
        ],
        out_specs=pl.BlockSpec(memory_space=vmem),
        scratch_shapes=[
            pltpu.VMEM((9, 3 * channels, channels), jnp.bfloat16),
            pltpu.VMEM((rows_in, span + 2 * LANE, 3 * channels), jnp.bfloat16),
            pltpu.VMEM((rows_in - 2, span, channels), jnp.float32),
            pltpu.SemaphoreType.DMA((3,)),
        ],
        compiler_params=pltpu.CompilerParams(vmem_limit_bytes=48 * 1024 * 1024),
    )(row_ok, xt, w_in_t, w_mid, w_pix)
    return out[:, :, :n_pix]


def local(latents, owners, conv_in, conv_mid, to_pixels):
    n = lax.axis_size("dev")
    assert n & (n - 1) == 0
    position = lax.axis_index("dev")
    groups, frames, height, width = latents.shape[1:]
    columns = width // ZC
    rows_dev = height // n
    bits = n.bit_length() - 1
    slot = reverse_bits(position, bits)
    steps = groups * frames
    assert columns < LANE

    x = jnp.transpose(latents[0], (2, 0, 1, 3))
    keep = owners == position
    x = jnp.where(keep[None, :, None, None], x, jnp.zeros_like(x))
    x = jnp.pad(x, ((HALO, HALO), (0, 0), (0, 0), (0, 0)))
    x = gather_rows(x, n, rows_dev, slot)

    rows_in = rows_dev + 2
    xt = x.reshape(rows_dev + 2 * HALO, steps, columns, ZC).transpose(0, 3, 1, 2)
    xt = jnp.pad(xt, ((0, 0), (0, 0), (2, 0), (0, LANE - columns)))
    xt = xt.reshape(rows_dev + 2 * HALO, ZC, (steps + 2) * LANE)
    row_of = slot * rows_dev - 1 + jnp.arange(rows_in)
    row_ok = ((row_of >= 0) & (row_of < height)).astype(jnp.float32)

    projected = decode(row_ok, xt, conv_in, conv_mid, to_pixels, columns)
    projected = projected.reshape(rows_dev, groups, frames, LANE, 2, 2, 3)[:, :, :, :columns]
    projected = projected.transpose(1, 2, 0, 4, 3, 5, 6)
    pixels = projected.reshape(groups, frames, 2 * rows_dev, 6 * columns).astype(jnp.bfloat16)
    return lax.ppermute(pixels, "dev", [(i, reverse_bits(i, bits)) for i in range(n)])


def solution(mesh):
    in_specs = (P(("stream", "dev"), None, None, None, None), P("stream"), P(), P(), P())
    out_specs = P("stream", None, "dev", None)
    return jax.shard_map(local, mesh=mesh, in_specs=in_specs, out_specs=out_specs, check_vma=False)
```

```python
import functools

import jax
import jax.numpy as jnp
from jax import lax
from jax.experimental import pallas as pl
from jax.experimental.pallas import tpu as pltpu
from jax.sharding import PartitionSpec as P

ZC = 16
HALO = 2

epsilon = 1e-06

def rms_scale(values):
    return values * lax.rsqrt(jnp.mean(values * values, axis=-1, keepdims=True) + epsilon)


def reverse_bits(value, bits):
    return sum(((value >> b) & 1) << (bits - 1 - b) for b in range(bits))


def gather_rows(x, n, rows_dev, slot):
    bits = n.bit_length() - 1
    for k in reversed(range(bits)):
        half = (1 << k) * rows_dev
        size = half + 2 * HALO
        bit = (slot >> k) & 1
        own = lax.dynamic_slice_in_dim(x, bit * half, size, 0)
        send = lax.dynamic_slice_in_dim(x, (1 - bit) * half, size, 0)
        flip = 1 << (bits - 1 - k)
        pairs = [(i, i ^ flip) for i in range(n)]
        x = own + lax.ppermute(send, "dev", pairs)
    return x


LANE = 128


def decode_kernel(columns, row_ok_ref, xt_ref, w_in_ref, w_hbm, w_pix_ref, out_ref, w_vmem, act_ref, center_ref, sem):
    rows_in = act_ref.shape[0]
    rows_out = rows_in - 2
    lead = 2 * LANE
    span = act_ref.shape[1] - lead
    channels = w_vmem.shape[2]
    taps = w_vmem.shape[0] // 3
    copies = [
        pltpu.make_async_copy(w_hbm.at[pl.ds(a * taps, taps)], w_vmem.at[pl.ds(a * taps, taps)], sem.at[a])
        for a in range(3)
    ]
    for copy in copies:
        copy.start()
    zeros = jnp.zeros((lead, 3 * channels), act_ref.dtype)
    for j in range(rows_in):
        act_ref[j, 0:lead, :] = zeros
    column = lax.broadcasted_iota(jnp.int32, (span, 1), 0) % LANE
    valid = column < columns
    w_in = w_in_ref[...]
    for j in range(rows_in):
        pieces = []
        for a in range(3):
            for b in range(3):
                src = xt_ref[j + b, :, a * LANE : a * LANE + span].astype(jnp.float32)
                for e in range(3):
                    shifted = src if e == 1 else pltpu.roll(src, (1 - e) % span, 1)
                    pieces.append(shifted.astype(jnp.bfloat16))
        patches = jnp.concatenate(pieces, axis=0)
        first_t = jnp.dot(w_in, patches, preferred_element_type=jnp.float32)
        first = jnp.where(valid, first_t.T, 0.0)
        if 1 <= j <= rows_out:
            center_ref[j - 1] = first
        scaled = first * lax.rsqrt(jnp.mean(first * first, axis=-1, keepdims=True) + epsilon)
        act = scaled / (1.0 + jnp.exp(-scaled)) * row_ok_ref[j]
        act_ref[j, lead:, 0:channels] = pltpu.roll(act, 1, 0).astype(act_ref.dtype)
        act_ref[j, lead:, channels : 2 * channels] = act.astype(act_ref.dtype)
        act_ref[j, lead:, 2 * channels :] = pltpu.roll(act, span - 1, 0).astype(act_ref.dtype)
    for jo in range(rows_out):
        acc = center_ref[jo]
        for a in range(3):
            if jo == 0:
                copies[a].wait()
            for b in range(3):
                piece = act_ref[jo + b, a * LANE : a * LANE + span, :]
                acc = acc + jnp.dot(piece, w_vmem[a * taps + b], preferred_element_type=jnp.float32)
        scale = lax.rsqrt(jnp.mean(acc * acc, axis=-1, keepdims=True) + epsilon)
        normed = (acc * scale).astype(jnp.bfloat16)
        out_ref[jo] = jnp.dot(normed, w_pix_ref[...], preferred_element_type=jnp.float32)


def decode(row_ok, xt, conv_in, conv_mid, to_pixels, columns):
    rows_in = xt.shape[0] - 2
    span = xt.shape[2] - 2 * LANE
    channels = conv_mid.shape[1]
    w_mid = conv_mid.reshape(9, 3 * channels, channels)
    w_in_t = conv_in.T
    n_pix = to_pixels.shape[1]
    w_pix = jnp.pad(to_pixels, ((0, 0), (0, LANE - n_pix)))
    vmem = pltpu.MemorySpace.VMEM
    out = pl.pallas_call(
        functools.partial(decode_kernel, columns),
        out_shape=jax.ShapeDtypeStruct((rows_in - 2, span, LANE), jnp.float32),
        in_specs=[
            pl.BlockSpec(memory_space=pltpu.MemorySpace.SMEM),
            pl.BlockSpec(memory_space=vmem),
            pl.BlockSpec(memory_space=vmem),
            pl.BlockSpec(memory_space=pl.ANY),
            pl.BlockSpec(memory_space=vmem),
        ],
        out_specs=pl.BlockSpec(memory_space=vmem),
        scratch_shapes=[
            pltpu.VMEM((9, 3 * channels, channels), jnp.bfloat16),
            pltpu.VMEM((rows_in, span + 2 * LANE, 3 * channels), jnp.bfloat16),
            pltpu.VMEM((rows_in - 2, span, channels), jnp.float32),
            pltpu.SemaphoreType.DMA((3,)),
        ],
        compiler_params=pltpu.CompilerParams(vmem_limit_bytes=48 * 1024 * 1024),
    )(row_ok, xt, w_in_t, w_mid, w_pix)
    return out[:, :, :n_pix]


def local(latents, owners, conv_in, conv_mid, to_pixels):
    n = lax.axis_size("dev")
    assert n & (n - 1) == 0
    position = lax.axis_index("dev")
    groups, frames, height, width = latents.shape[1:]
    columns = width // ZC
    rows_dev = height // n
    bits = n.bit_length() - 1
    slot = reverse_bits(position, bits)
    steps = groups * frames
    assert columns < LANE

    x = jnp.transpose(latents[0], (2, 0, 1, 3))
    keep = owners == position
    x = jnp.where(keep[None, :, None, None], x, jnp.zeros_like(x))
    x = jnp.pad(x, ((HALO, HALO), (0, 0), (0, 0), (0, 0)))
    x = gather_rows(x, n, rows_dev, slot)

    rows_in = rows_dev + 2
    xt = x.reshape(rows_dev + 2 * HALO, steps, columns, ZC).transpose(0, 3, 1, 2)
    xt = jnp.pad(xt, ((0, 0), (0, 0), (2, 0), (0, LANE - columns)))
    xt = xt.reshape(rows_dev + 2 * HALO, ZC, (steps + 2) * LANE)
    row_of = slot * rows_dev - 1 + jnp.arange(rows_in)
    row_ok = ((row_of >= 0) & (row_of < height)).astype(jnp.float32)

    projected = decode(row_ok, xt, conv_in, conv_mid, to_pixels, columns)
    projected = projected.reshape(rows_dev, groups, frames, LANE, 2, 2, 3)[:, :, :, :columns]
    projected = projected.transpose(1, 2, 0, 4, 3, 5, 6)
    pixels = projected.reshape(groups, frames, 2 * rows_dev, 6 * columns).astype(jnp.bfloat16)
    return lax.ppermute(pixels, "dev", [(i, reverse_bits(i, bits)) for i in range(n)])


def solution(mesh):
    in_specs = (P(("stream", "dev"), None, None, None, None), P("stream"), P(), P(), P())
    out_specs = P("stream", None, "dev", None)
    return jax.shard_map(local, mesh=mesh, in_specs=in_specs, out_specs=out_specs, check_vma=False)
```

```python
import functools

import jax
import jax.numpy as jnp
from jax import lax
from jax.experimental import pallas as pl
from jax.experimental.pallas import tpu as pltpu
from jax.sharding import PartitionSpec as P

ZC = 16
HALO = 2

epsilon = 1e-06

def rms_scale(values):
    return values * lax.rsqrt(jnp.mean(values * values, axis=-1, keepdims=True) + epsilon)


def reverse_bits(value, bits):
    return sum(((value >> b) & 1) << (bits - 1 - b) for b in range(bits))


def gather_rows(x, n, rows_dev, slot):
    bits = n.bit_length() - 1
    for k in reversed(range(bits)):
        half = (1 << k) * rows_dev
        size = half + 2 * HALO
        bit = (slot >> k) & 1
        own = lax.dynamic_slice_in_dim(x, bit * half, size, 0)
        send = lax.dynamic_slice_in_dim(x, (1 - bit) * half, size, 0)
        flip = 1 << (bits - 1 - k)
        pairs = [(i, i ^ flip) for i in range(n)]
        x = own + lax.ppermute(send, "dev", pairs)
    return x


LANE = 128


def decode_kernel(columns, row_ok_ref, xt_ref, w_in_ref, w_hbm, w_pix_ref, out_ref, w_vmem, act_ref, center_ref, sem):
    rows_in = act_ref.shape[0]
    rows_out = rows_in - 2
    lead = 2 * LANE
    span = act_ref.shape[1] - lead
    channels = w_vmem.shape[2]
    taps = w_vmem.shape[0] // 3
    copies = [
        pltpu.make_async_copy(w_hbm.at[pl.ds(a * taps, taps)], w_vmem.at[pl.ds(a * taps, taps)], sem.at[a])
        for a in range(3)
    ]
    for copy in copies:
        copy.start()
    zeros = jnp.zeros((lead, 3 * channels), act_ref.dtype)
    for j in range(rows_in):
        act_ref[j, 0:lead, :] = zeros
    column = lax.broadcasted_iota(jnp.int32, (span, 1), 0) % LANE
    valid = column < columns
    w_in = w_in_ref[...]
    for j in range(rows_in):
        pieces = []
        for a in range(3):
            for b in range(3):
                src = xt_ref[j + b, :, a * LANE : a * LANE + span].astype(jnp.float32)
                for e in range(3):
                    shifted = src if e == 1 else pltpu.roll(src, (1 - e) % span, 1)
                    pieces.append(shifted.astype(jnp.bfloat16))
        patches = jnp.concatenate(pieces, axis=0)
        first_t = jnp.dot(w_in, patches, preferred_element_type=jnp.float32)
        first = jnp.where(valid, first_t.T, 0.0)
        if 1 <= j <= rows_out:
            center_ref[j - 1] = first
        scaled = first * lax.rsqrt(jnp.mean(first * first, axis=-1, keepdims=True) + epsilon)
        act = scaled / (1.0 + jnp.exp(-scaled)) * row_ok_ref[j]
        act_ref[j, lead:, 0:channels] = pltpu.roll(act, 1, 0).astype(act_ref.dtype)
        act_ref[j, lead:, channels : 2 * channels] = act.astype(act_ref.dtype)
        act_ref[j, lead:, 2 * channels :] = pltpu.roll(act, span - 1, 0).astype(act_ref.dtype)
    for jo in range(rows_out):
        acc = center_ref[jo]
        for a in range(3):
            if jo == 0:
                copies[a].wait()
            for b in range(3):
                piece = act_ref[jo + b, a * LANE : a * LANE + span, :]
                acc = acc + jnp.dot(piece, w_vmem[a * taps + b], preferred_element_type=jnp.float32)
        scale = lax.rsqrt(jnp.mean(acc * acc, axis=-1, keepdims=True) + epsilon)
        normed = (acc * scale).astype(jnp.bfloat16)
        out_ref[jo] = jnp.dot(normed, w_pix_ref[...], preferred_element_type=jnp.float32).astype(out_ref.dtype)


def decode(row_ok, xt, conv_in, conv_mid, to_pixels, columns):
    rows_in = xt.shape[0] - 2
    span = xt.shape[2] - 2 * LANE
    channels = conv_mid.shape[1]
    w_mid = conv_mid.reshape(9, 3 * channels, channels)
    w_in_t = conv_in.T
    n_pix = to_pixels.shape[1]
    w_pix = jnp.pad(to_pixels, ((0, 0), (0, LANE - n_pix)))
    vmem = pltpu.MemorySpace.VMEM
    out = pl.pallas_call(
        functools.partial(decode_kernel, columns),
        out_shape=jax.ShapeDtypeStruct((rows_in - 2, span, LANE), jnp.bfloat16),
        in_specs=[
            pl.BlockSpec(memory_space=pltpu.MemorySpace.SMEM),
            pl.BlockSpec(memory_space=vmem),
            pl.BlockSpec(memory_space=vmem),
            pl.BlockSpec(memory_space=pl.ANY),
            pl.BlockSpec(memory_space=vmem),
        ],
        out_specs=pl.BlockSpec(memory_space=vmem),
        scratch_shapes=[
            pltpu.VMEM((9, 3 * channels, channels), jnp.bfloat16),
            pltpu.VMEM((rows_in, span + 2 * LANE, 3 * channels), jnp.bfloat16),
            pltpu.VMEM((rows_in - 2, span, channels), jnp.float32),
            pltpu.SemaphoreType.DMA((3,)),
        ],
        compiler_params=pltpu.CompilerParams(vmem_limit_bytes=48 * 1024 * 1024),
    )(row_ok, xt, w_in_t, w_mid, w_pix)
    return out[:, :, :n_pix]


def local(latents, owners, conv_in, conv_mid, to_pixels):
    n = lax.axis_size("dev")
    assert n & (n - 1) == 0
    position = lax.axis_index("dev")
    groups, frames, height, width = latents.shape[1:]
    columns = width // ZC
    rows_dev = height // n
    bits = n.bit_length() - 1
    slot = reverse_bits(position, bits)
    steps = groups * frames
    assert columns < LANE

    x = jnp.transpose(latents[0], (2, 0, 1, 3))
    keep = owners == position
    x = jnp.where(keep[None, :, None, None], x, jnp.zeros_like(x))
    x = jnp.pad(x, ((HALO, HALO), (0, 0), (0, 0), (0, 0)))
    x = gather_rows(x, n, rows_dev, slot)

    rows_in = rows_dev + 2
    xt = x.reshape(rows_dev + 2 * HALO, steps, columns, ZC).transpose(0, 3, 1, 2)
    xt = jnp.pad(xt, ((0, 0), (0, 0), (2, 0), (0, LANE - columns)))
    xt = xt.reshape(rows_dev + 2 * HALO, ZC, (steps + 2) * LANE)
    row_of = slot * rows_dev - 1 + jnp.arange(rows_in)
    row_ok = ((row_of >= 0) & (row_of < height)).astype(jnp.float32)

    projected = decode(row_ok, xt, conv_in, conv_mid, to_pixels, columns)
    projected = projected.reshape(rows_dev, groups, frames, LANE, 2, 2, 3)[:, :, :, :columns]
    projected = projected.transpose(1, 2, 0, 4, 3, 5, 6)
    pixels = projected.reshape(groups, frames, 2 * rows_dev, 6 * columns)
    return lax.ppermute(pixels, "dev", [(i, reverse_bits(i, bits)) for i in range(n)])


def solution(mesh):
    in_specs = (P(("stream", "dev"), None, None, None, None), P("stream"), P(), P(), P())
    out_specs = P("stream", None, "dev", None)
    return jax.shard_map(local, mesh=mesh, in_specs=in_specs, out_specs=out_specs, check_vma=False)
```

```python
import functools

import jax
import jax.numpy as jnp
from jax import lax
from jax.experimental import pallas as pl
from jax.experimental.pallas import tpu as pltpu
from jax.sharding import PartitionSpec as P

ZC = 16
HALO = 2

epsilon = 1e-06

def rms_scale(values):
    return values * lax.rsqrt(jnp.mean(values * values, axis=-1, keepdims=True) + epsilon)


def reverse_bits(value, bits):
    return sum(((value >> b) & 1) << (bits - 1 - b) for b in range(bits))


def gather_rows(x, n, rows_dev, slot, axis=0):
    bits = n.bit_length() - 1
    for k in reversed(range(bits)):
        half = (1 << k) * rows_dev
        size = half + 2 * HALO
        bit = (slot >> k) & 1
        own = lax.dynamic_slice_in_dim(x, bit * half, size, axis)
        send = lax.dynamic_slice_in_dim(x, (1 - bit) * half, size, axis)
        flip = 1 << (bits - 1 - k)
        pairs = [(i, i ^ flip) for i in range(n)]
        x = own + lax.ppermute(send, "dev", pairs)
    return x


LANE = 128


def decode_kernel(columns, row_ok_ref, xt_ref, w_in_ref, w_hbm, w_pix_ref, out_ref, w_vmem, act_ref, center_ref, sem):
    rows_in = act_ref.shape[0]
    rows_out = rows_in - 2
    lead = 2 * LANE
    span = act_ref.shape[1] - lead
    channels = w_vmem.shape[2]
    taps = w_vmem.shape[0] // 3
    copies = [
        pltpu.make_async_copy(w_hbm.at[pl.ds(a * taps, taps)], w_vmem.at[pl.ds(a * taps, taps)], sem.at[a])
        for a in range(3)
    ]
    for copy in copies:
        copy.start()
    zeros = jnp.zeros((lead, 3 * channels), act_ref.dtype)
    for j in range(rows_in):
        act_ref[j, 0:lead, :] = zeros
    column = lax.broadcasted_iota(jnp.int32, (span, 1), 0) % LANE
    valid = column < columns
    w_in = w_in_ref[...]
    for j in range(rows_in):
        pieces = []
        for a in range(3):
            for b in range(3):
                src = xt_ref[j + b, :, a * LANE : a * LANE + span].astype(jnp.float32)
                for e in range(3):
                    shifted = src if e == 1 else pltpu.roll(src, (1 - e) % span, 1)
                    pieces.append(shifted.astype(jnp.bfloat16))
        patches = jnp.concatenate(pieces, axis=0)
        first_t = jnp.dot(w_in, patches, preferred_element_type=jnp.float32)
        first = jnp.where(valid, first_t.T, 0.0)
        if 1 <= j <= rows_out:
            center_ref[j - 1] = first
        scaled = first * lax.rsqrt(jnp.mean(first * first, axis=-1, keepdims=True) + epsilon)
        act = scaled / (1.0 + jnp.exp(-scaled)) * row_ok_ref[j]
        act_ref[j, lead:, 0:channels] = pltpu.roll(act, 1, 0).astype(act_ref.dtype)
        act_ref[j, lead:, channels : 2 * channels] = act.astype(act_ref.dtype)
        act_ref[j, lead:, 2 * channels :] = pltpu.roll(act, span - 1, 0).astype(act_ref.dtype)
    for jo in range(rows_out):
        acc = center_ref[jo]
        for a in range(3):
            if jo == 0:
                copies[a].wait()
            for b in range(3):
                piece = act_ref[jo + b, a * LANE : a * LANE + span, :]
                acc = acc + jnp.dot(piece, w_vmem[a * taps + b], preferred_element_type=jnp.float32)
        scale = lax.rsqrt(jnp.mean(acc * acc, axis=-1, keepdims=True) + epsilon)
        normed = (acc * scale).astype(jnp.bfloat16)
        out_ref[jo] = jnp.dot(normed, w_pix_ref[...], preferred_element_type=jnp.float32).astype(out_ref.dtype)


def decode(row_ok, xt, conv_in, conv_mid, to_pixels, columns):
    rows_in = xt.shape[0] - 2
    span = xt.shape[2] - 2 * LANE
    channels = conv_mid.shape[1]
    w_mid = conv_mid.reshape(9, 3 * channels, channels)
    w_in_t = conv_in.T
    n_pix = to_pixels.shape[1]
    w_pix = jnp.pad(to_pixels, ((0, 0), (0, LANE - n_pix)))
    vmem = pltpu.MemorySpace.VMEM
    out = pl.pallas_call(
        functools.partial(decode_kernel, columns),
        out_shape=jax.ShapeDtypeStruct((rows_in - 2, span, LANE), jnp.bfloat16),
        in_specs=[
            pl.BlockSpec(memory_space=pltpu.MemorySpace.SMEM),
            pl.BlockSpec(memory_space=vmem),
            pl.BlockSpec(memory_space=vmem),
            pl.BlockSpec(memory_space=pl.ANY),
            pl.BlockSpec(memory_space=vmem),
        ],
        out_specs=pl.BlockSpec(memory_space=vmem),
        scratch_shapes=[
            pltpu.VMEM((9, 3 * channels, channels), jnp.bfloat16),
            pltpu.VMEM((rows_in, span + 2 * LANE, 3 * channels), jnp.bfloat16),
            pltpu.VMEM((rows_in - 2, span, channels), jnp.float32),
            pltpu.SemaphoreType.DMA((3,)),
        ],
        compiler_params=pltpu.CompilerParams(vmem_limit_bytes=48 * 1024 * 1024),
    )(row_ok, xt, w_in_t, w_mid, w_pix)
    return out[:, :, :n_pix]


def local(latents, owners, conv_in, conv_mid, to_pixels):
    n = lax.axis_size("dev")
    assert n & (n - 1) == 0
    position = lax.axis_index("dev")
    groups, frames, height, width = latents.shape[1:]
    columns = width // ZC
    rows_dev = height // n
    bits = n.bit_length() - 1
    slot = reverse_bits(position, bits)
    steps = groups * frames
    assert columns < LANE

    keep = owners == position
    x = jnp.where(keep[:, None, None, None], latents[0], jnp.zeros_like(latents[0]))
    x = jnp.pad(x, ((0, 0), (0, 0), (HALO, HALO), (0, 0)))
    x = gather_rows(x, n, rows_dev, slot, axis=2)

    rows_in = rows_dev + 2
    xt = x.reshape(steps, rows_dev + 2 * HALO, columns, ZC).transpose(1, 3, 0, 2)
    xt = jnp.pad(xt, ((0, 0), (0, 0), (2, 0), (0, LANE - columns)))
    xt = xt.reshape(rows_dev + 2 * HALO, ZC, (steps + 2) * LANE)
    row_of = slot * rows_dev - 1 + jnp.arange(rows_in)
    row_ok = ((row_of >= 0) & (row_of < height)).astype(jnp.float32)

    projected = decode(row_ok, xt, conv_in, conv_mid, to_pixels, columns)
    projected = projected.reshape(rows_dev, groups, frames, LANE, 2, 2, 3)[:, :, :, :columns]
    projected = projected.transpose(1, 2, 0, 4, 3, 5, 6)
    pixels = projected.reshape(groups, frames, 2 * rows_dev, 6 * columns)
    return lax.ppermute(pixels, "dev", [(i, reverse_bits(i, bits)) for i in range(n)])


def solution(mesh):
    in_specs = (P(("stream", "dev"), None, None, None, None), P("stream"), P(), P(), P())
    out_specs = P("stream", None, "dev", None)
    return jax.shard_map(local, mesh=mesh, in_specs=in_specs, out_specs=out_specs, check_vma=False)
```

```python
import functools

import jax
import jax.numpy as jnp
from jax import lax
from jax.experimental import pallas as pl
from jax.experimental.pallas import tpu as pltpu
from jax.sharding import PartitionSpec as P

ZC = 16
HALO = 2

epsilon = 1e-06

def rms_scale(values):
    return values * lax.rsqrt(jnp.mean(values * values, axis=-1, keepdims=True) + epsilon)


def reverse_bits(value, bits):
    return sum(((value >> b) & 1) << (bits - 1 - b) for b in range(bits))


def gather_rows(x, n, rows_dev, slot, axis=0):
    bits = n.bit_length() - 1
    for k in reversed(range(bits)):
        half = (1 << k) * rows_dev
        size = half + 2 * HALO
        bit = (slot >> k) & 1
        own = lax.dynamic_slice_in_dim(x, bit * half, size, axis)
        send = lax.dynamic_slice_in_dim(x, (1 - bit) * half, size, axis)
        flip = 1 << (bits - 1 - k)
        pairs = [(i, i ^ flip) for i in range(n)]
        x = own + lax.ppermute(send, "dev", pairs)
    return x


LANE = 128


def decode_kernel(columns, row_ok_ref, xt_ref, w_in_ref, w_hbm, w_pix_ref, out_ref, w_vmem, act_ref, center_ref, sem):
    rows_in = act_ref.shape[0]
    rows_out = rows_in - 2
    lead = 2 * LANE
    span = act_ref.shape[1] - lead
    channels = w_vmem.shape[2]
    taps = w_vmem.shape[0] // 3
    copies = [
        pltpu.make_async_copy(w_hbm.at[pl.ds(a * taps, taps)], w_vmem.at[pl.ds(a * taps, taps)], sem.at[a])
        for a in range(3)
    ]
    for copy in copies:
        copy.start()
    zeros = jnp.zeros((lead, 3 * channels), act_ref.dtype)
    for j in range(rows_in):
        act_ref[j, 0:lead, :] = zeros
    column = lax.broadcasted_iota(jnp.int32, (span, 1), 0) % LANE
    valid = column < columns
    w_in = w_in_ref[...]
    for j in range(rows_in):
        pieces = []
        for a in range(3):
            for b in range(3):
                for e in range(3):
                    pieces.append(xt_ref[j + b, e, :, a * LANE : a * LANE + span])
        patches = jnp.concatenate(pieces, axis=0)
        first_t = jnp.dot(w_in, patches, preferred_element_type=jnp.float32)
        first = jnp.where(valid, first_t.T, 0.0)
        if 1 <= j <= rows_out:
            center_ref[j - 1] = first
        scaled = first * lax.rsqrt(jnp.mean(first * first, axis=-1, keepdims=True) + epsilon)
        act = scaled / (1.0 + jnp.exp(-scaled)) * row_ok_ref[j]
        act_ref[j, lead:, 0:channels] = pltpu.roll(act, 1, 0).astype(act_ref.dtype)
        act_ref[j, lead:, channels : 2 * channels] = act.astype(act_ref.dtype)
        act_ref[j, lead:, 2 * channels :] = pltpu.roll(act, span - 1, 0).astype(act_ref.dtype)
    for jo in range(rows_out):
        acc = center_ref[jo]
        for a in range(3):
            if jo == 0:
                copies[a].wait()
            for b in range(3):
                piece = act_ref[jo + b, a * LANE : a * LANE + span, :]
                acc = acc + jnp.dot(piece, w_vmem[a * taps + b], preferred_element_type=jnp.float32)
        scale = lax.rsqrt(jnp.mean(acc * acc, axis=-1, keepdims=True) + epsilon)
        normed = (acc * scale).astype(jnp.bfloat16)
        out_ref[jo] = jnp.dot(normed, w_pix_ref[...], preferred_element_type=jnp.float32).astype(out_ref.dtype)


def decode(row_ok, xt, conv_in, conv_mid, to_pixels, columns):
    rows_in = xt.shape[0] - 2
    span = xt.shape[3] - 2 * LANE
    channels = conv_mid.shape[1]
    w_mid = conv_mid.reshape(9, 3 * channels, channels)
    w_in_t = conv_in.T
    n_pix = to_pixels.shape[1]
    w_pix = jnp.pad(to_pixels, ((0, 0), (0, LANE - n_pix)))
    vmem = pltpu.MemorySpace.VMEM
    out = pl.pallas_call(
        functools.partial(decode_kernel, columns),
        out_shape=jax.ShapeDtypeStruct((rows_in - 2, span, LANE), jnp.bfloat16),
        in_specs=[
            pl.BlockSpec(memory_space=pltpu.MemorySpace.SMEM),
            pl.BlockSpec(memory_space=vmem),
            pl.BlockSpec(memory_space=vmem),
            pl.BlockSpec(memory_space=pl.ANY),
            pl.BlockSpec(memory_space=vmem),
        ],
        out_specs=pl.BlockSpec(memory_space=vmem),
        scratch_shapes=[
            pltpu.VMEM((9, 3 * channels, channels), jnp.bfloat16),
            pltpu.VMEM((rows_in, span + 2 * LANE, 3 * channels), jnp.bfloat16),
            pltpu.VMEM((rows_in - 2, span, channels), jnp.float32),
            pltpu.SemaphoreType.DMA((3,)),
        ],
        compiler_params=pltpu.CompilerParams(vmem_limit_bytes=48 * 1024 * 1024),
    )(row_ok, xt, w_in_t, w_mid, w_pix)
    return out[:, :, :n_pix]


def local(latents, owners, conv_in, conv_mid, to_pixels):
    n = lax.axis_size("dev")
    assert n & (n - 1) == 0
    position = lax.axis_index("dev")
    groups, frames, height, width = latents.shape[1:]
    columns = width // ZC
    rows_dev = height // n
    bits = n.bit_length() - 1
    slot = reverse_bits(position, bits)
    steps = groups * frames
    assert columns < LANE

    keep = owners == position
    x = jnp.where(keep[:, None, None, None], latents[0], jnp.zeros_like(latents[0]))
    x = jnp.pad(x, ((0, 0), (0, 0), (HALO, HALO), (0, 0)))
    x = gather_rows(x, n, rows_dev, slot, axis=2)

    rows_in = rows_dev + 2
    xt = x.reshape(steps, rows_dev + 2 * HALO, columns, ZC).transpose(1, 3, 0, 2)
    xt = jnp.pad(xt, ((0, 0), (0, 0), (2, 0), (0, LANE - columns)))
    xt = xt.reshape(rows_dev + 2 * HALO, ZC, (steps + 2) * LANE)
    xt = jnp.stack([jnp.roll(xt, 1 - e, axis=2) for e in range(3)], axis=1)
    row_of = slot * rows_dev - 1 + jnp.arange(rows_in)
    row_ok = ((row_of >= 0) & (row_of < height)).astype(jnp.float32)

    projected = decode(row_ok, xt, conv_in, conv_mid, to_pixels, columns)
    projected = projected.reshape(rows_dev, groups, frames, LANE, 2, 2, 3)[:, :, :, :columns]
    projected = projected.transpose(1, 2, 0, 4, 3, 5, 6)
    pixels = projected.reshape(groups, frames, 2 * rows_dev, 6 * columns)
    return lax.ppermute(pixels, "dev", [(i, reverse_bits(i, bits)) for i in range(n)])


def solution(mesh):
    in_specs = (P(("stream", "dev"), None, None, None, None), P("stream"), P(), P(), P())
    out_specs = P("stream", None, "dev", None)
    return jax.shard_map(local, mesh=mesh, in_specs=in_specs, out_specs=out_specs, check_vma=False)
```

```python
import functools

import jax
import jax.numpy as jnp
from jax import lax
from jax.experimental import pallas as pl
from jax.experimental.pallas import tpu as pltpu
from jax.sharding import PartitionSpec as P

ZC = 16
HALO = 2

epsilon = 1e-06

def rms_scale(values):
    return values * lax.rsqrt(jnp.mean(values * values, axis=-1, keepdims=True) + epsilon)


def reverse_bits(value, bits):
    return sum(((value >> b) & 1) << (bits - 1 - b) for b in range(bits))


def gather_rows(x, n, rows_dev, slot, axis=0):
    bits = n.bit_length() - 1
    for k in reversed(range(bits)):
        half = (1 << k) * rows_dev
        size = half + 2 * HALO
        bit = (slot >> k) & 1
        own = lax.dynamic_slice_in_dim(x, bit * half, size, axis)
        send = lax.dynamic_slice_in_dim(x, (1 - bit) * half, size, axis)
        flip = 1 << (bits - 1 - k)
        pairs = [(i, i ^ flip) for i in range(n)]
        x = own + lax.ppermute(send, "dev", pairs)
    return x


LANE = 128


def decode_kernel(columns, row_ok_ref, xt_ref, w_in_ref, w_hbm, w_pix_ref, out_ref, w_vmem, act_ref, center_ref, sem):
    rows_in = act_ref.shape[0]
    rows_out = rows_in - 2
    lead = 2 * LANE
    span = act_ref.shape[1] - lead
    channels = w_vmem.shape[2]
    taps = w_vmem.shape[0] // 3
    copies = [
        pltpu.make_async_copy(w_hbm.at[pl.ds(a * taps, taps)], w_vmem.at[pl.ds(a * taps, taps)], sem.at[a])
        for a in range(3)
    ]
    for copy in copies:
        copy.start()
    zeros = jnp.zeros((lead, 3 * channels), act_ref.dtype)
    for j in range(rows_in):
        act_ref[j, 0:lead, :] = zeros
    column = lax.broadcasted_iota(jnp.int32, (span, 1), 0) % LANE
    valid = column < columns
    w_in = w_in_ref[...]
    columns_all = []
    for j in range(rows_in):
        pieces = []
        for a in range(3):
            for b in range(3):
                for e in range(3):
                    pieces.append(xt_ref[j + b, e, :, a * LANE : a * LANE + span])
        columns_all.append(jnp.concatenate(pieces, axis=0))
    first_all = jnp.dot(w_in, jnp.concatenate(columns_all, axis=1), preferred_element_type=jnp.float32)
    for j in range(rows_in):
        first = jnp.where(valid, first_all[:, j * span : (j + 1) * span].T, 0.0)
        if 1 <= j <= rows_out:
            center_ref[j - 1] = first
        scaled = first * lax.rsqrt(jnp.mean(first * first, axis=-1, keepdims=True) + epsilon)
        act = scaled / (1.0 + jnp.exp(-scaled)) * row_ok_ref[j]
        act_ref[j, lead:, 0:channels] = pltpu.roll(act, 1, 0).astype(act_ref.dtype)
        act_ref[j, lead:, channels : 2 * channels] = act.astype(act_ref.dtype)
        act_ref[j, lead:, 2 * channels :] = pltpu.roll(act, span - 1, 0).astype(act_ref.dtype)
    for jo in range(rows_out):
        acc = center_ref[jo]
        for a in range(3):
            if jo == 0:
                copies[a].wait()
            for b in range(3):
                piece = act_ref[jo + b, a * LANE : a * LANE + span, :]
                acc = acc + jnp.dot(piece, w_vmem[a * taps + b], preferred_element_type=jnp.float32)
        scale = lax.rsqrt(jnp.mean(acc * acc, axis=-1, keepdims=True) + epsilon)
        normed = (acc * scale).astype(jnp.bfloat16)
        out_ref[jo] = jnp.dot(normed, w_pix_ref[...], preferred_element_type=jnp.float32).astype(out_ref.dtype)


def decode(row_ok, xt, conv_in, conv_mid, to_pixels, columns):
    rows_in = xt.shape[0] - 2
    span = xt.shape[3] - 2 * LANE
    channels = conv_mid.shape[1]
    w_mid = conv_mid.reshape(9, 3 * channels, channels)
    w_in_t = conv_in.T
    n_pix = to_pixels.shape[1]
    w_pix = jnp.pad(to_pixels, ((0, 0), (0, LANE - n_pix)))
    vmem = pltpu.MemorySpace.VMEM
    out = pl.pallas_call(
        functools.partial(decode_kernel, columns),
        out_shape=jax.ShapeDtypeStruct((rows_in - 2, span, LANE), jnp.bfloat16),
        in_specs=[
            pl.BlockSpec(memory_space=pltpu.MemorySpace.SMEM),
            pl.BlockSpec(memory_space=vmem),
            pl.BlockSpec(memory_space=vmem),
            pl.BlockSpec(memory_space=pl.ANY),
            pl.BlockSpec(memory_space=vmem),
        ],
        out_specs=pl.BlockSpec(memory_space=vmem),
        scratch_shapes=[
            pltpu.VMEM((9, 3 * channels, channels), jnp.bfloat16),
            pltpu.VMEM((rows_in, span + 2 * LANE, 3 * channels), jnp.bfloat16),
            pltpu.VMEM((rows_in - 2, span, channels), jnp.float32),
            pltpu.SemaphoreType.DMA((3,)),
        ],
        compiler_params=pltpu.CompilerParams(vmem_limit_bytes=48 * 1024 * 1024),
    )(row_ok, xt, w_in_t, w_mid, w_pix)
    return out[:, :, :n_pix]


def local(latents, owners, conv_in, conv_mid, to_pixels):
    n = lax.axis_size("dev")
    assert n & (n - 1) == 0
    position = lax.axis_index("dev")
    groups, frames, height, width = latents.shape[1:]
    columns = width // ZC
    rows_dev = height // n
    bits = n.bit_length() - 1
    slot = reverse_bits(position, bits)
    steps = groups * frames
    assert columns < LANE

    keep = owners == position
    x = jnp.where(keep[:, None, None, None], latents[0], jnp.zeros_like(latents[0]))
    x = jnp.pad(x, ((0, 0), (0, 0), (HALO, HALO), (0, 0)))
    x = gather_rows(x, n, rows_dev, slot, axis=2)

    rows_in = rows_dev + 2
    xt = x.reshape(steps, rows_dev + 2 * HALO, columns, ZC).transpose(1, 3, 0, 2)
    xt = jnp.pad(xt, ((0, 0), (0, 0), (2, 0), (0, LANE - columns)))
    xt = xt.reshape(rows_dev + 2 * HALO, ZC, (steps + 2) * LANE)
    xt = jnp.stack([jnp.roll(xt, 1 - e, axis=2) for e in range(3)], axis=1)
    row_of = slot * rows_dev - 1 + jnp.arange(rows_in)
    row_ok = ((row_of >= 0) & (row_of < height)).astype(jnp.float32)

    projected = decode(row_ok, xt, conv_in, conv_mid, to_pixels, columns)
    projected = projected.reshape(rows_dev, groups, frames, LANE, 2, 2, 3)[:, :, :, :columns]
    projected = projected.transpose(1, 2, 0, 4, 3, 5, 6)
    pixels = projected.reshape(groups, frames, 2 * rows_dev, 6 * columns)
    return lax.ppermute(pixels, "dev", [(i, reverse_bits(i, bits)) for i in range(n)])


def solution(mesh):
    in_specs = (P(("stream", "dev"), None, None, None, None), P("stream"), P(), P(), P())
    out_specs = P("stream", None, "dev", None)
    return jax.shard_map(local, mesh=mesh, in_specs=in_specs, out_specs=out_specs, check_vma=False)
```

```python
import functools

import jax
import jax.numpy as jnp
from jax import lax
from jax.experimental import pallas as pl
from jax.experimental.pallas import tpu as pltpu
from jax.sharding import PartitionSpec as P

ZC = 16
HALO = 2

epsilon = 1e-06

def rms_scale(values):
    return values * lax.rsqrt(jnp.mean(values * values, axis=-1, keepdims=True) + epsilon)


def reverse_bits(value, bits):
    return sum(((value >> b) & 1) << (bits - 1 - b) for b in range(bits))


def gather_rows(x, n, rows_dev, slot, axis=0):
    bits = n.bit_length() - 1
    for k in reversed(range(bits)):
        half = (1 << k) * rows_dev
        size = half + 2 * HALO
        bit = (slot >> k) & 1
        own = lax.dynamic_slice_in_dim(x, bit * half, size, axis)
        send = lax.dynamic_slice_in_dim(x, (1 - bit) * half, size, axis)
        flip = 1 << (bits - 1 - k)
        pairs = [(i, i ^ flip) for i in range(n)]
        x = own + lax.ppermute(send, "dev", pairs)
    return x


LANE = 128


def decode_kernel(columns, row_ok_ref, xt_ref, w_in_ref, w_hbm, w_pix_ref, out_ref, w_vmem, act_ref, center_ref, sem):
    rows_in = act_ref.shape[0]
    rows_out = rows_in - 2
    lead = 2 * LANE
    span = act_ref.shape[1] - lead
    channels = w_vmem.shape[2]
    taps = w_vmem.shape[0] // 3
    copies = [
        pltpu.make_async_copy(w_hbm.at[pl.ds(a * taps, taps)], w_vmem.at[pl.ds(a * taps, taps)], sem.at[a])
        for a in range(3)
    ]
    for copy in copies:
        copy.start()
    zeros = jnp.zeros((lead, 3 * channels), act_ref.dtype)
    for j in range(rows_in):
        act_ref[j, 0:lead, :] = zeros
    column = lax.broadcasted_iota(jnp.int32, (span, 1), 0) % LANE
    valid = column < columns
    w_in = w_in_ref[...]
    columns_all = []
    for j in range(rows_in):
        pieces = []
        for a in range(3):
            for b in range(3):
                for e in range(3):
                    pieces.append(xt_ref[j + b, e, :, a * LANE : a * LANE + span])
        columns_all.append(jnp.concatenate(pieces, axis=0))
    first_all = jnp.dot(w_in, jnp.concatenate(columns_all, axis=1), preferred_element_type=jnp.float32)
    for j in range(rows_in):
        first = jnp.where(valid, first_all[:, j * span : (j + 1) * span].T, 0.0)
        if 1 <= j <= rows_out:
            center_ref[j - 1] = first
        scaled = first * lax.rsqrt(jnp.mean(first * first, axis=-1, keepdims=True) + epsilon)
        act = scaled / (1.0 + jnp.exp(-scaled)) * row_ok_ref[j]
        act_ref[j, lead:, 0:channels] = pltpu.roll(act, 1, 0).astype(act_ref.dtype)
        act_ref[j, lead:, channels : 2 * channels] = act.astype(act_ref.dtype)
        act_ref[j, lead:, 2 * channels :] = pltpu.roll(act, span - 1, 0).astype(act_ref.dtype)
    for jo in range(rows_out):
        acc = center_ref[jo]
        for a in range(3):
            if jo == 0:
                copies[a].wait()
            for b in range(3):
                piece = act_ref[jo + b, a * LANE : a * LANE + span, :]
                acc = acc + jnp.dot(piece, w_vmem[a * taps + b], preferred_element_type=jnp.float32)
        scale = lax.rsqrt(jnp.mean(acc * acc, axis=-1, keepdims=True) + epsilon)
        normed = (acc * scale).astype(jnp.bfloat16)
        out_ref[jo] = jnp.dot(normed, w_pix_ref[...], preferred_element_type=jnp.float32).astype(out_ref.dtype)


def decode(row_ok, xt, conv_in, conv_mid, to_pixels, columns):
    rows_in = xt.shape[0] - 2
    span = xt.shape[3] - 2 * LANE
    channels = conv_mid.shape[1]
    w_mid = conv_mid.reshape(9, 3 * channels, channels)
    w_in_t = conv_in.T
    n_pix = to_pixels.shape[1]
    w_pix = jnp.pad(to_pixels, ((0, 0), (0, LANE - n_pix)))
    vmem = pltpu.MemorySpace.VMEM
    out = pl.pallas_call(
        functools.partial(decode_kernel, columns),
        out_shape=jax.ShapeDtypeStruct((rows_in - 2, span, LANE), jnp.bfloat16),
        in_specs=[
            pl.BlockSpec(memory_space=pltpu.MemorySpace.SMEM),
            pl.BlockSpec(memory_space=vmem),
            pl.BlockSpec(memory_space=vmem),
            pl.BlockSpec(memory_space=pl.ANY),
            pl.BlockSpec(memory_space=vmem),
        ],
        out_specs=pl.BlockSpec(memory_space=vmem),
        scratch_shapes=[
            pltpu.VMEM((9, 3 * channels, channels), jnp.bfloat16),
            pltpu.VMEM((rows_in, span + 2 * LANE, 3 * channels), jnp.bfloat16),
            pltpu.VMEM((rows_in - 2, span, channels), jnp.float32),
            pltpu.SemaphoreType.DMA((3,)),
        ],
        compiler_params=pltpu.CompilerParams(vmem_limit_bytes=48 * 1024 * 1024),
    )(row_ok, xt, w_in_t, w_mid, w_pix)
    return out[:, :, :n_pix]


def local(latents, owners, conv_in, conv_mid, to_pixels):
    n = lax.axis_size("dev")
    assert n & (n - 1) == 0
    position = lax.axis_index("dev")
    groups, frames, height, width = latents.shape[1:]
    columns = width // ZC
    rows_dev = height // n
    bits = n.bit_length() - 1
    slot = reverse_bits(position, bits)
    steps = groups * frames
    assert columns < LANE

    zero = jnp.zeros_like(latents[0, 0])
    x = jnp.stack([jnp.where(owners[g] == position, latents[0, g], zero) for g in range(groups)])
    x = jnp.pad(x, ((0, 0), (0, 0), (HALO, HALO), (0, 0)))
    x = gather_rows(x, n, rows_dev, slot, axis=2)

    rows_in = rows_dev + 2
    xt = x.reshape(steps, rows_dev + 2 * HALO, columns, ZC).transpose(1, 3, 0, 2)
    xt = jnp.pad(xt, ((0, 0), (0, 0), (2, 0), (0, LANE - columns)))
    xt = xt.reshape(rows_dev + 2 * HALO, ZC, (steps + 2) * LANE)
    xt = jnp.stack([jnp.roll(xt, 1 - e, axis=2) for e in range(3)], axis=1)
    row_of = slot * rows_dev - 1 + jnp.arange(rows_in)
    row_ok = ((row_of >= 0) & (row_of < height)).astype(jnp.float32)

    projected = decode(row_ok, xt, conv_in, conv_mid, to_pixels, columns)
    projected = projected.reshape(rows_dev, groups, frames, LANE, 2, 2, 3)[:, :, :, :columns]
    projected = projected.transpose(1, 2, 0, 4, 3, 5, 6)
    pixels = projected.reshape(groups, frames, 2 * rows_dev, 6 * columns)
    return lax.ppermute(pixels, "dev", [(i, reverse_bits(i, bits)) for i in range(n)])


def solution(mesh):
    in_specs = (P(("stream", "dev"), None, None, None, None), P("stream"), P(), P(), P())
    out_specs = P("stream", None, "dev", None)
    return jax.shard_map(local, mesh=mesh, in_specs=in_specs, out_specs=out_specs, check_vma=False)
```

```python
import functools

import jax
import jax.numpy as jnp
from jax import lax
from jax.experimental import pallas as pl
from jax.experimental.pallas import tpu as pltpu
from jax.sharding import PartitionSpec as P

ZC = 16
HALO = 2

epsilon = 1e-06

def rms_scale(values):
    return values * lax.rsqrt(jnp.mean(values * values, axis=-1, keepdims=True) + epsilon)


def reverse_bits(value, bits):
    return sum(((value >> b) & 1) << (bits - 1 - b) for b in range(bits))


def gather_rows(x, n, rows_dev, slot, axis=0):
    bits = n.bit_length() - 1
    for k in reversed(range(bits)):
        half = (1 << k) * rows_dev
        size = half + 2 * HALO
        bit = (slot >> k) & 1
        own = lax.dynamic_slice_in_dim(x, bit * half, size, axis)
        send = lax.dynamic_slice_in_dim(x, (1 - bit) * half, size, axis)
        flip = 1 << (bits - 1 - k)
        pairs = [(i, i ^ flip) for i in range(n)]
        x = own + lax.ppermute(send, "dev", pairs)
    return x


LANE = 128


def decode_kernel(columns, row_ok_ref, xt_ref, w_in_ref, w_hbm, w_pix_ref, out_ref, w_vmem, act_ref, center_ref, sem):
    rows_in = act_ref.shape[0]
    rows_out = rows_in - 2
    lead = 2 * LANE
    span = act_ref.shape[1] - lead
    channels = w_vmem.shape[2]
    taps = w_vmem.shape[0] // 3
    copies = [
        pltpu.make_async_copy(w_hbm.at[pl.ds(a * taps, taps)], w_vmem.at[pl.ds(a * taps, taps)], sem.at[a])
        for a in range(3)
    ]
    for copy in copies:
        copy.start()
    zeros = jnp.zeros((lead, 3 * channels), act_ref.dtype)
    for j in range(rows_in):
        act_ref[j, 0:lead, :] = zeros
    column = lax.broadcasted_iota(jnp.int32, (span, 1), 0) % LANE
    valid = column < columns
    w_in = w_in_ref[...]
    for j in range(rows_in):
        pieces = []
        for a in range(3):
            for b in range(3):
                for e in range(3):
                    pieces.append(xt_ref[j + b, e, :, a * LANE : a * LANE + span])
        patches = jnp.concatenate(pieces, axis=0)
        first_t = lax.dot_general(w_in, patches, (((0,), (0,)), ((), ())), preferred_element_type=jnp.float32)
        first = jnp.where(valid, first_t.T, 0.0)
        if 1 <= j <= rows_out:
            center_ref[j - 1] = first
        scaled = first * lax.rsqrt(jnp.mean(first * first, axis=-1, keepdims=True) + epsilon)
        act = scaled / (1.0 + jnp.exp(-scaled)) * row_ok_ref[j]
        act_ref[j, lead:, 0:channels] = pltpu.roll(act, 1, 0).astype(act_ref.dtype)
        act_ref[j, lead:, channels : 2 * channels] = act.astype(act_ref.dtype)
        act_ref[j, lead:, 2 * channels :] = pltpu.roll(act, span - 1, 0).astype(act_ref.dtype)
    for jo in range(rows_out):
        acc = center_ref[jo]
        for a in range(3):
            if jo == 0:
                copies[a].wait()
            for b in range(3):
                piece = act_ref[jo + b, a * LANE : a * LANE + span, :]
                acc = acc + jnp.dot(piece, w_vmem[a * taps + b], preferred_element_type=jnp.float32)
        scale = lax.rsqrt(jnp.mean(acc * acc, axis=-1, keepdims=True) + epsilon)
        normed = (acc * scale).astype(jnp.bfloat16)
        out_ref[jo] = jnp.dot(normed, w_pix_ref[...], preferred_element_type=jnp.float32).astype(out_ref.dtype)


def decode(row_ok, xt, conv_in, conv_mid, to_pixels, columns):
    rows_in = xt.shape[0] - 2
    span = xt.shape[3] - 2 * LANE
    channels = conv_mid.shape[1]
    w_mid = conv_mid.reshape(9, 3 * channels, channels)
    n_pix = to_pixels.shape[1]
    w_pix = jnp.pad(to_pixels, ((0, 0), (0, LANE - n_pix)))
    vmem = pltpu.MemorySpace.VMEM
    out = pl.pallas_call(
        functools.partial(decode_kernel, columns),
        out_shape=jax.ShapeDtypeStruct((rows_in - 2, span, LANE), jnp.bfloat16),
        in_specs=[
            pl.BlockSpec(memory_space=pltpu.MemorySpace.SMEM),
            pl.BlockSpec(memory_space=vmem),
            pl.BlockSpec(memory_space=vmem),
            pl.BlockSpec(memory_space=pl.ANY),
            pl.BlockSpec(memory_space=vmem),
        ],
        out_specs=pl.BlockSpec(memory_space=vmem),
        scratch_shapes=[
            pltpu.VMEM((9, 3 * channels, channels), jnp.bfloat16),
            pltpu.VMEM((rows_in, span + 2 * LANE, 3 * channels), jnp.bfloat16),
            pltpu.VMEM((rows_in - 2, span, channels), jnp.float32),
            pltpu.SemaphoreType.DMA((3,)),
        ],
        compiler_params=pltpu.CompilerParams(vmem_limit_bytes=48 * 1024 * 1024),
    )(row_ok, xt, conv_in, w_mid, w_pix)
    return out[:, :, :n_pix]


def local(latents, owners, conv_in, conv_mid, to_pixels):
    n = lax.axis_size("dev")
    assert n & (n - 1) == 0
    position = lax.axis_index("dev")
    groups, frames, height, width = latents.shape[1:]
    columns = width // ZC
    rows_dev = height // n
    bits = n.bit_length() - 1
    slot = reverse_bits(position, bits)
    steps = groups * frames
    assert columns < LANE

    keep = owners == position
    x = jnp.where(keep[:, None, None, None], latents[0], jnp.zeros_like(latents[0]))
    x = jnp.pad(x, ((0, 0), (0, 0), (HALO, HALO), (0, 0)))
    x = gather_rows(x, n, rows_dev, slot, axis=2)

    rows_in = rows_dev + 2
    xt = x.reshape(steps, rows_dev + 2 * HALO, columns, ZC).transpose(1, 3, 0, 2)
    xt = jnp.pad(xt, ((0, 0), (0, 0), (2, 0), (0, LANE - columns)))
    xt = xt.reshape(rows_dev + 2 * HALO, ZC, (steps + 2) * LANE)
    xt = jnp.stack([jnp.roll(xt, 1 - e, axis=2) for e in range(3)], axis=1)
    row_of = slot * rows_dev - 1 + jnp.arange(rows_in)
    row_ok = ((row_of >= 0) & (row_of < height)).astype(jnp.float32)

    projected = decode(row_ok, xt, conv_in, conv_mid, to_pixels, columns)
    projected = projected.reshape(rows_dev, groups, frames, LANE, 2, 2, 3)[:, :, :, :columns]
    projected = projected.transpose(1, 2, 0, 4, 3, 5, 6)
    pixels = projected.reshape(groups, frames, 2 * rows_dev, 6 * columns)
    return lax.ppermute(pixels, "dev", [(i, reverse_bits(i, bits)) for i in range(n)])


def solution(mesh):
    in_specs = (P(("stream", "dev"), None, None, None, None), P("stream"), P(), P(), P())
    out_specs = P("stream", None, "dev", None)
    return jax.shard_map(local, mesh=mesh, in_specs=in_specs, out_specs=out_specs, check_vma=False)
```

```python
import functools

import jax
import jax.numpy as jnp
from jax import lax
from jax.experimental import pallas as pl
from jax.experimental.pallas import tpu as pltpu
from jax.sharding import PartitionSpec as P

ZC = 16
HALO = 2

epsilon = 1e-06

def rms_scale(values):
    return values * lax.rsqrt(jnp.mean(values * values, axis=-1, keepdims=True) + epsilon)


def reverse_bits(value, bits):
    return sum(((value >> b) & 1) << (bits - 1 - b) for b in range(bits))


def gather_rows(x, n, rows_dev, slot, axis=0):
    bits = n.bit_length() - 1
    for k in reversed(range(bits)):
        half = (1 << k) * rows_dev
        size = half + 2 * HALO
        bit = (slot >> k) & 1
        own = lax.dynamic_slice_in_dim(x, bit * half, size, axis)
        send = lax.dynamic_slice_in_dim(x, (1 - bit) * half, size, axis)
        flip = 1 << (bits - 1 - k)
        pairs = [(i, i ^ flip) for i in range(n)]
        x = own + lax.ppermute(send, "dev", pairs)
    return x


LANE = 128


def decode_kernel(columns, row_ok_ref, xt_ref, w_in_ref, w_hbm, w_pix_ref, out_ref, w_vmem, act_ref, center_ref, sem):
    rows_in = act_ref.shape[0]
    rows_out = rows_in - 2
    lead = 2 * LANE
    span = act_ref.shape[1] - lead
    channels = w_vmem.shape[2]
    taps = w_vmem.shape[0] // 3
    copies = [pltpu.make_async_copy(w_hbm.at[t], w_vmem.at[t], sem.at[t]) for t in range(w_vmem.shape[0])]
    for copy in copies:
        copy.start()
    zeros = jnp.zeros((lead, 3 * channels), act_ref.dtype)
    for j in range(rows_in):
        act_ref[j, 0:lead, :] = zeros
    column = lax.broadcasted_iota(jnp.int32, (span, 1), 0) % LANE
    valid = column < columns
    w_in = w_in_ref[...]
    for j in range(rows_in):
        pieces = []
        for a in range(3):
            for b in range(3):
                for e in range(3):
                    pieces.append(xt_ref[j + b, e, :, a * LANE : a * LANE + span])
        patches = jnp.concatenate(pieces, axis=0)
        first_t = jnp.dot(w_in, patches, preferred_element_type=jnp.float32)
        first = jnp.where(valid, first_t.T, 0.0)
        if 1 <= j <= rows_out:
            center_ref[j - 1] = first
        scaled = first * lax.rsqrt(jnp.mean(first * first, axis=-1, keepdims=True) + epsilon)
        act = scaled / (1.0 + jnp.exp(-scaled)) * row_ok_ref[j]
        act_ref[j, lead:, 0:channels] = pltpu.roll(act, 1, 0).astype(act_ref.dtype)
        act_ref[j, lead:, channels : 2 * channels] = act.astype(act_ref.dtype)
        act_ref[j, lead:, 2 * channels :] = pltpu.roll(act, span - 1, 0).astype(act_ref.dtype)
    for jo in range(rows_out):
        acc = center_ref[jo]
        for a in range(3):
            for b in range(3):
                if jo == 0:
                    copies[a * taps + b].wait()
                piece = act_ref[jo + b, a * LANE : a * LANE + span, :]
                acc = acc + jnp.dot(piece, w_vmem[a * taps + b], preferred_element_type=jnp.float32)
        scale = lax.rsqrt(jnp.mean(acc * acc, axis=-1, keepdims=True) + epsilon)
        normed = (acc * scale).astype(jnp.bfloat16)
        out_ref[jo] = jnp.dot(normed, w_pix_ref[...], preferred_element_type=jnp.float32).astype(out_ref.dtype)


def decode(row_ok, xt, conv_in, conv_mid, to_pixels, columns):
    rows_in = xt.shape[0] - 2
    span = xt.shape[3] - 2 * LANE
    channels = conv_mid.shape[1]
    w_mid = conv_mid.reshape(9, 3 * channels, channels)
    w_in_t = conv_in.T
    n_pix = to_pixels.shape[1]
    w_pix = jnp.pad(to_pixels, ((0, 0), (0, LANE - n_pix)))
    vmem = pltpu.MemorySpace.VMEM
    out = pl.pallas_call(
        functools.partial(decode_kernel, columns),
        out_shape=jax.ShapeDtypeStruct((rows_in - 2, span, LANE), jnp.bfloat16),
        in_specs=[
            pl.BlockSpec(memory_space=pltpu.MemorySpace.SMEM),
            pl.BlockSpec(memory_space=vmem),
            pl.BlockSpec(memory_space=vmem),
            pl.BlockSpec(memory_space=pl.ANY),
            pl.BlockSpec(memory_space=vmem),
        ],
        out_specs=pl.BlockSpec(memory_space=vmem),
        scratch_shapes=[
            pltpu.VMEM((9, 3 * channels, channels), jnp.bfloat16),
            pltpu.VMEM((rows_in, span + 2 * LANE, 3 * channels), jnp.bfloat16),
            pltpu.VMEM((rows_in - 2, span, channels), jnp.float32),
            pltpu.SemaphoreType.DMA((9,)),
        ],
        compiler_params=pltpu.CompilerParams(vmem_limit_bytes=48 * 1024 * 1024),
    )(row_ok, xt, w_in_t, w_mid, w_pix)
    return out[:, :, :n_pix]


def local(latents, owners, conv_in, conv_mid, to_pixels):
    n = lax.axis_size("dev")
    assert n & (n - 1) == 0
    position = lax.axis_index("dev")
    groups, frames, height, width = latents.shape[1:]
    columns = width // ZC
    rows_dev = height // n
    bits = n.bit_length() - 1
    slot = reverse_bits(position, bits)
    steps = groups * frames
    assert columns < LANE

    keep = owners == position
    x = jnp.where(keep[:, None, None, None], latents[0], jnp.zeros_like(latents[0]))
    x = jnp.pad(x, ((0, 0), (0, 0), (HALO, HALO), (0, 0)))
    x = gather_rows(x, n, rows_dev, slot, axis=2)

    rows_in = rows_dev + 2
    xt = x.reshape(steps, rows_dev + 2 * HALO, columns, ZC).transpose(1, 3, 0, 2)
    xt = jnp.pad(xt, ((0, 0), (0, 0), (2, 0), (0, LANE - columns)))
    xt = xt.reshape(rows_dev + 2 * HALO, ZC, (steps + 2) * LANE)
    xt = jnp.stack([jnp.roll(xt, 1 - e, axis=2) for e in range(3)], axis=1)
    row_of = slot * rows_dev - 1 + jnp.arange(rows_in)
    row_ok = ((row_of >= 0) & (row_of < height)).astype(jnp.float32)

    projected = decode(row_ok, xt, conv_in, conv_mid, to_pixels, columns)
    projected = projected.reshape(rows_dev, groups, frames, LANE, 2, 2, 3)[:, :, :, :columns]
    projected = projected.transpose(1, 2, 0, 4, 3, 5, 6)
    pixels = projected.reshape(groups, frames, 2 * rows_dev, 6 * columns)
    return lax.ppermute(pixels, "dev", [(i, reverse_bits(i, bits)) for i in range(n)])


def solution(mesh):
    in_specs = (P(("stream", "dev"), None, None, None, None), P("stream"), P(), P(), P())
    out_specs = P("stream", None, "dev", None)
    return jax.shard_map(local, mesh=mesh, in_specs=in_specs, out_specs=out_specs, check_vma=False)
```
